128 devices in a mesh: req: 16 (over y, z), mlp: 8 (over x, core).
Axes of the slice: x: 4, y: 4, z: 4, core: 2. Of those that a mesh axis runs over, the one named last changes fastest.
Arguments:
- tokens: bfloat16 [32768, 1536], P(('req', 'mlp')), may hold values from -6 to 6
- attn_gain: float32 [1536], replicated, may hold values from 0.1 to 1.9
- w_query: bfloat16 [1536, 1536], replicated, may hold values from -0.15625 to 0.15625
- w_keyval: bfloat16 [1536, 256], replicated, may hold values from -0.15625 to 0.15625
- w_out: bfloat16 [1536, 1536], replicated, may hold values from -0.15625 to 0.15625
- ffn_gain: float32 [1536], replicated, may hold values from 0.1 to 1.9
- w_gate: bfloat16 [1536, 4608], P('req', 'mlp'), may hold values from -0.15625 to 0.15625
- w_up: bfloat16 [1536, 4608], P('req', 'mlp'), may hold values from -0.15625 to 0.15625
- w_down: bfloat16 [1536, 4608], P('req', 'mlp'), may hold values from -0.09375 to 0.09375
- prefix_kv: bfloat16 [2, 128, 512, 256], P(None, 'req'), may hold values from -60 to 60, as said below
- own_prefix: bfloat16 [16, 512, 256], P('req'), may hold values from -60 to 60, as said below
- leaf_parent: int32 [16], replicated, may hold values from 0 to 127
- node_parent: int32 [128], replicated, may hold values from 0 to 127
- seg_lengths: int32 [3, 128], replicated, may hold values from 1 to 512
Outputs:
- layer_out: bfloat16 [32768, 1536], P(('req', 'mlp'))
The draws below stay inside these ranges and needn't reach their ends.
Inputs may be any that keep to these rules, and one draw needn't show every extreme that they name: `prefix_kv`: columns below 128 are keys, the rest values. `own_prefix`: columns below 128 are keys, the rest values.
All inputs are finite; a program needn't handle non-finite values.
Results may differ from the reference program's by a relative error of at most 0.018.
Values may be sent and summed in bfloat16 or wider, within the bound.
No kernel may reach another device: no remote copies, remote signals or barrier semaphores. Data moves between devices by JAX's collectives and lax.ppermute only.
A program may use at most 192 MiB of HBM per device.

```python
import math
import jax
import jax.numpy as jnp
import numpy as np
from jax import lax

D = 1536
HEADS = 12
HD = 128
FF = 4608
WINDOW = 1024
SEG = 512
QTOK = 2048
REQS = 16
NODES = 128
TOKENS = 32768
N_MLP = 8


def kv_block(key, shape):
    key_one, key_two = jax.random.split(key, 2)
    half_shape = shape[:-1] + (HD,)
    keys_part = jax.random.normal(key_one, half_shape, jnp.float32)
    vals_part = jax.random.normal(key_two, half_shape, jnp.float32)
    return jnp.clip(jnp.concatenate([keys_part, vals_part], -1), -60.0, 60.0).astype(jnp.bfloat16)


def draw_prefix_kv(key, part):
    return kv_block(jax.random.fold_in(key, 11), (2, NODES, SEG, 2 * HD))


def draw_own_prefix(key, part):
    return kv_block(jax.random.fold_in(key, 23), (REQS, SEG, 2 * HD))


def touch_ends(result, stream_key, low, high):
    place = [jax.random.randint(jax.random.fold_in(stream_key, axis), (), 0, length) for axis, length in enumerate(result.shape)]
    main_axis = result.shape.index(max(result.shape))
    beside = place[:main_axis] + [(place[main_axis] + 1) % result.shape[main_axis]] + place[main_axis + 1:]
    return result.at[tuple(place)].set(low).at[tuple(beside)].set(high)


def shard_levels(key, dims, pieces, smallest, top_value):
    factor_of = 1.0
    for dim, blocks in pieces:
        draws = jax.random.uniform(jax.random.fold_in(jax.random.fold_in(key, 6), dim), (blocks,), jnp.float32, smallest / len(pieces), top_value / len(pieces))
        factor_of = factor_of * jnp.repeat(jnp.exp(draws), dims[dim] // blocks).reshape((-1,) + (1,) * (len(dims) - 1 - dim))
    return factor_of


def rank_table(count, slope):
    portions = [(1 << 20) // math.isqrt(grade ** slope) + 1 for grade in range(1, count + 1)]
    spread = 1 + sum(portions) // (1 << 30)
    return np.cumsum(np.array([max(1, weight // spread) for weight in portions]))


def ranked(stream_key, extent, amount, slope):
    listing = rank_table(amount, slope)
    pick = jax.random.randint(jax.random.fold_in(stream_key, 1), extent, 0, int(listing[amount - 1]))
    standing = jnp.searchsorted(jnp.asarray(listing, jnp.int32), pick, side="right")
    return jax.random.permutation(jax.random.fold_in(stream_key, 2), amount)[standing].astype(jnp.int32)


def bell_draw(key, extent, spread, most, cuts=(), held_as=jnp.bfloat16):
    drawn = jax.random.normal(key, extent, jnp.float32) * spread
    if len(cuts) > 0:
        drawn = shard_levels(key, extent, cuts, -0.22, 0.18) * drawn
    return jnp.clip(drawn, min=-most, max=most).astype(held_as)


def setup_inputs(seed: int = 0) -> dict:
    splits = jax.random.split(jax.random.key(seed), 15)
    return {
        "tokens": bell_draw(splits[0], (TOKENS, D), 1.0, 6.0, ((0, 128),)),
        "attn_gain": jnp.clip(1.0 + 0.18 * jax.random.normal(splits[1], (D,), jnp.float32), 0.1, 1.9),
        "w_query": bell_draw(splits[2], (D, HEADS * HD), D ** -0.5, 0.15625),
        "w_keyval": bell_draw(splits[3], (D, 2 * HD), D ** -0.5, 0.15625),
        "w_out": bell_draw(splits[4], (HEADS * HD, D), (HEADS * HD) ** -0.5, 0.15625),
        "ffn_gain": jnp.clip(1.0 + 0.18 * jax.random.normal(splits[5], (D,), jnp.float32), 0.1, 1.9),
        "w_gate": bell_draw(splits[6], (D, FF), D ** -0.5, 0.15625, ((0, 16), (1, 8))),
        "w_up": bell_draw(splits[7], (D, FF), D ** -0.5, 0.15625, ((0, 16), (1, 8))),
        "w_down": bell_draw(splits[8], (D, FF), FF ** -0.5, 0.09375, ((0, 16), (1, 8))),
        "prefix_kv": draw_prefix_kv(jax.random.fold_in(splits[14], 71), 0),
        "own_prefix": draw_own_prefix(jax.random.fold_in(splits[14], 71), 0),
        "leaf_parent": touch_ends(ranked(splits[11], (REQS,), NODES, 2), jax.random.fold_in(splits[11], 3), 0, NODES - 1).astype(jnp.int32),
        "node_parent": touch_ends(ranked(splits[12], (NODES,), NODES, 2), jax.random.fold_in(splits[12], 3), 0, NODES - 1).astype(jnp.int32),
        "seg_lengths": touch_ends(jax.random.randint(splits[13], (3, NODES), 1, SEG + 1), jax.random.fold_in(splits[13], 1), 1, SEG).astype(jnp.int32),
    }


EPS = 1e-06

def rounded(values):
    return lax.optimization_barrier(values.astype(jnp.bfloat16))

def rms_scale(values, gain):
    wide = values.astype(jnp.float32)
    return wide * lax.rsqrt(lax.optimization_barrier(jnp.mean(wide * wide, axis=-1, keepdims=True)) + EPS) * gain

def rotate(values, where_at):
    half_dim = values.shape[-1] // 2
    freqs = 10000.0 ** (-jnp.arange(half_dim, dtype=jnp.float32) / half_dim)
    angles = where_at.astype(jnp.float32)[:, None] * freqs[None, :]
    cosine = jnp.cos(angles)[:, None, :]
    sine = jnp.sin(angles)[:, None, :]
    first = values[..., :half_dim]
    second = values[..., half_dim:]
    return jnp.concatenate([first * cosine - second * sine, first * sine + second * cosine], -1)

def reference(tokens, attn_gain, w_query, w_keyval, w_out, ffn_gain, w_gate, w_up, w_down, prefix_kv, own_prefix, leaf_parent, node_parent, seg_lengths):
    normed = rounded(rms_scale(tokens, attn_gain))
    query_all = jnp.dot(normed, w_query, preferred_element_type=jnp.float32)
    keyval_all = jnp.dot(normed, w_keyval, preferred_element_type=jnp.float32)
    offsets = jnp.arange(SEG, dtype=jnp.int32)
    steps_new = jnp.arange(QTOK, dtype=jnp.int32)

    def one_request(request):
        leaf = leaf_parent[request]
        upper = node_parent[leaf]
        len_zero = seg_lengths[0, upper]
        len_one = seg_lengths[1, leaf]
        len_two = seg_lengths[2, request]
        total = len_zero + len_one + len_two
        query_at = total + steps_new
        start_row = (request * QTOK).astype(jnp.int32)
        rows_query = lax.dynamic_slice_in_dim(query_all, start_row, QTOK, 0).reshape(QTOK, HEADS, HD)
        queries = rounded(rotate(rows_query, query_at) * HD ** (-0.5))
        rows_keyval = lax.dynamic_slice_in_dim(keyval_all, start_row, QTOK, 0)
        new_keys = rounded(rotate(rows_keyval[:, None, :HD], query_at)[:, 0])
        new_vals = rounded(rows_keyval[:, HD:])
        cached = jnp.concatenate([prefix_kv[0, upper], prefix_kv[1, leaf], own_prefix[request]], 0)
        key_rows = jnp.concatenate([cached[:, :HD], new_keys], 0)
        val_rows = jnp.concatenate([cached[:, HD:], new_vals], 0)
        key_at = jnp.concatenate([offsets, len_zero + offsets, len_zero + len_one + offsets, query_at], 0)
        key_live = jnp.concatenate([offsets < len_zero, offsets < len_one, offsets < len_two, jnp.ones((QTOK,), dtype=bool)], 0)
        scores = jnp.einsum('thd,kd->thk', queries.astype(jnp.float32), key_rows.astype(jnp.float32))
        spacing = query_at[:, None] - key_at[None, :]
        allowed = (key_live[None, :] & (spacing >= 0) & (spacing < WINDOW))[:, None, :]
        top = lax.optimization_barrier(jnp.max(jnp.where(allowed, scores, -jnp.inf), axis=-1, keepdims=True))
        weights = jnp.where(allowed, jnp.exp(scores - top), 0.0)
        denom = lax.optimization_barrier(jnp.sum(weights, axis=-1))
        mixed = jnp.einsum('thk,kd->thd', rounded(weights).astype(jnp.float32), val_rows.astype(jnp.float32))
        return (mixed / denom[..., None]).reshape(QTOK, HEADS * HD).astype(jnp.bfloat16)
    contexts = lax.map(one_request, jnp.arange(REQS, dtype=jnp.int32)).reshape(TOKENS, HEADS * HD)
    attn_out = jnp.dot(contexts, w_out, preferred_element_type=jnp.float32)
    resid = rounded(tokens.astype(jnp.float32) + attn_out)
    ffn_in = rounded(rms_scale(resid, ffn_gain))
    gate = jnp.dot(ffn_in, w_gate, preferred_element_type=jnp.float32)
    upward = jnp.dot(ffn_in, w_up, preferred_element_type=jnp.float32)
    hidden = rounded(jax.nn.gelu(gate, approximate=True) * upward)
    slice_width = FF // N_MLP

    def add_slice(summed, index):
        first_col = (index * slice_width).astype(jnp.int32)
        cols = lax.dynamic_slice_in_dim(hidden, first_col, slice_width, 1)
        down_cols = lax.dynamic_slice_in_dim(w_down, first_col, slice_width, 1)
        partial_sum = lax.dot_general(cols, down_cols, (((1,), (1,)), ((), ())), preferred_element_type=jnp.float32)
        return (summed + rounded(partial_sum).astype(jnp.float32), None)
    summed, unused = lax.scan(add_slice, jnp.zeros((TOKENS, D), jnp.float32), jnp.arange(N_MLP, dtype=jnp.int32))
    return (resid.astype(jnp.float32) + summed).astype(jnp.bfloat16)
```

```python
import jax
import jax.numpy as jnp
from jax import lax
from jax.sharding import PartitionSpec as P

HEADS = 12
HD = 128
WINDOW = 1024


EPS = 1e-06


def rms_scale(values, gain):
    wide = values.astype(jnp.float32)
    return wide * lax.rsqrt(jnp.mean(wide * wide, axis=-1, keepdims=True) + EPS) * gain


def rotate(values, where_at):
    half_dim = values.shape[-1] // 2
    freqs = 10000.0 ** (-jnp.arange(half_dim, dtype=jnp.float32) / half_dim)
    angles = where_at.astype(jnp.float32)[:, None] * freqs[None, :]
    cosine = jnp.cos(angles)[:, None, :]
    sine = jnp.sin(angles)[:, None, :]
    first = values[..., :half_dim]
    second = values[..., half_dim:]
    return jnp.concatenate([first * cosine - second * sine, first * sine + second * cosine], -1)


def body(
    tokens,
    attn_gain,
    w_query,
    w_keyval,
    w_out,
    ffn_gain,
    w_gate,
    w_up,
    w_down,
    prefix_kv,
    own_prefix,
    leaf_parent,
    node_parent,
    seg_lengths,
):
    tok_rows = tokens.shape[0]
    mine = lax.axis_index("req")
    n_mlp = lax.axis_size("mlp")
    position_group = lax.axis_index("mlp")
    node_dev = prefix_kv.shape[1]
    seg_slot = prefix_kv.shape[2]
    share = seg_slot // n_mlp
    leaf = leaf_parent[mine]
    upper = node_parent[leaf]
    len_zero = seg_lengths[0, upper]
    len_one = seg_lengths[1, leaf]
    len_two = seg_lengths[2, mine]
    total = len_zero + len_one + len_two

    ff_cols = w_gate.shape[1]
    packed = lax.all_gather(
        jnp.concatenate([w_gate, w_up, w_down], 1), "req", axis=0, tiled=True
    )
    gate_full = packed[:, :ff_cols]
    up_full = packed[:, ff_cols : 2 * ff_cols]
    down_full = packed[:, 2 * ff_cols :]

    level_zero = node_parent[leaf_parent]
    wanted = jnp.stack([level_zero, leaf_parent], 1)
    local_slot = wanted % node_dev
    my_rows = lax.dynamic_slice_in_dim(prefix_kv, position_group * share, share, 2)
    outgoing = my_rows[jnp.arange(2)[None, :], local_slot]
    arrived = lax.all_to_all(outgoing, "req", split_axis=0, concat_axis=0, tiled=True)
    owners = wanted[mine] // node_dev
    my_part = arrived[owners, jnp.arange(2)]
    levels = lax.all_gather(my_part, "mlp", axis=1, tiled=True)

    query_at = total + position_group * tok_rows + jnp.arange(tok_rows, dtype=jnp.int32)
    normed = rms_scale(tokens, attn_gain).astype(jnp.bfloat16)
    query_full = jnp.dot(normed, w_query, preferred_element_type=jnp.float32).reshape(
        tok_rows, HEADS, HD
    )
    queries = (rotate(query_full, query_at) * HD ** (-0.5)).astype(jnp.bfloat16)
    keyval_full = jnp.dot(normed, w_keyval, preferred_element_type=jnp.float32)
    new_keys = rotate(keyval_full[:, None, :HD], query_at)[:, 0].astype(jnp.bfloat16)
    new_vals = keyval_full[:, HD:].astype(jnp.bfloat16)
    new_keyval = jnp.concatenate([new_keys, new_vals], 1)
    piece = lax.all_gather(new_keyval, "mlp", axis=0, tiled=True)

    seq_len = 3 * seg_slot + piece.shape[0]
    seq = jnp.zeros((seq_len, piece.shape[1]), jnp.bfloat16)
    seq = lax.dynamic_update_slice(seq, levels[0], (0, 0))
    seq = lax.dynamic_update_slice(seq, levels[1], (len_zero, 0))
    seq = lax.dynamic_update_slice(seq, own_prefix[0], (len_zero + len_one, 0))
    seq = lax.dynamic_update_slice(seq, piece, (total, 0))
    span = WINDOW + tok_rows
    first = jnp.clip(total + position_group * tok_rows - WINDOW, 0, seq_len - span)
    window = lax.dynamic_slice_in_dim(seq, first, span, 0)
    key_at = first + jnp.arange(span, dtype=jnp.int32)
    spacing = query_at[:, None] - key_at[None, :]
    allowed = ((spacing >= 0) & (spacing < WINDOW))[:, None, :]
    scores = jnp.einsum(
        "thd,kd->thk", queries, window[:, :HD], preferred_element_type=jnp.float32
    )
    top = jnp.max(jnp.where(allowed, scores, -jnp.inf), axis=-1, keepdims=True)
    weights = jnp.where(allowed, jnp.exp(scores - top), 0.0)
    denom = jnp.sum(weights, axis=-1)
    mixed = jnp.einsum(
        "thk,kd->thd",
        weights.astype(jnp.bfloat16),
        window[:, HD:],
        preferred_element_type=jnp.float32,
    )
    context = (mixed / denom[..., None]).reshape(tok_rows, HEADS * HD).astype(jnp.bfloat16)
    attn_out = jnp.dot(context, w_out, preferred_element_type=jnp.float32)
    resid = (tokens.astype(jnp.float32) + attn_out).astype(jnp.bfloat16)
    ffn_in = rms_scale(resid, ffn_gain).astype(jnp.bfloat16)
    all_rows = lax.all_gather(ffn_in, "mlp", axis=0, tiled=True)
    gate = jnp.dot(all_rows, gate_full, preferred_element_type=jnp.float32)
    upward = jnp.dot(all_rows, up_full, preferred_element_type=jnp.float32)
    hidden = (jax.nn.gelu(gate, approximate=True) * upward).astype(jnp.bfloat16)
    summed = lax.psum_scatter(
        lax.dot_general(
            hidden, down_full, (((1,), (1,)), ((), ())), preferred_element_type=jnp.float32
        ).astype(jnp.bfloat16),
        "mlp",
        scatter_dimension=0,
        tiled=True,
    ).astype(jnp.float32)
    return (resid.astype(jnp.float32) + summed).astype(jnp.bfloat16)


def solution(mesh):
    return jax.shard_map(
        body,
        mesh=mesh,
        in_specs=(
            P(("req", "mlp"), None),
            P(),
            P(),
            P(),
            P(),
            P(),
            P("req", "mlp"),
            P("req", "mlp"),
            P("req", "mlp"),
            P(None, "req", None, None),
            P("req", None, None),
            P(),
            P(),
            P(),
        ),
        out_specs=P(("req", "mlp"), None),
        check_vma=False,
    )
```

```python
import jax
import jax.numpy as jnp
from jax import lax
from jax.sharding import PartitionSpec as P

HEADS = 12
HD = 128
WINDOW = 1024


EPS = 1e-06


def rms_scale(values, gain):
    wide = values.astype(jnp.float32)
    return wide * lax.rsqrt(jnp.mean(wide * wide, axis=-1, keepdims=True) + EPS) * gain


def rotate(values, where_at):
    half_dim = values.shape[-1] // 2
    freqs = 10000.0 ** (-jnp.arange(half_dim, dtype=jnp.float32) / half_dim)
    angles = where_at.astype(jnp.float32)[:, None] * freqs[None, :]
    cosine = jnp.cos(angles)[:, None, :]
    sine = jnp.sin(angles)[:, None, :]
    first = values[..., :half_dim]
    second = values[..., half_dim:]
    return jnp.concatenate([first * cosine - second * sine, first * sine + second * cosine], -1)


def body(
    tokens,
    attn_gain,
    w_query,
    w_keyval,
    w_out,
    ffn_gain,
    w_gate,
    w_up,
    w_down,
    prefix_kv,
    own_prefix,
    leaf_parent,
    node_parent,
    seg_lengths,
):
    tok_rows = tokens.shape[0]
    mine = lax.axis_index("req")
    n_core = lax.axis_size("core")
    n_mlp = lax.axis_size("x") * n_core
    position_group = lax.axis_index("x") * n_core + lax.axis_index("core")
    node_dev = prefix_kv.shape[1]
    seg_slot = prefix_kv.shape[2]
    share = seg_slot // n_mlp
    leaf = leaf_parent[mine]
    upper = node_parent[leaf]
    len_zero = seg_lengths[0, upper]
    len_one = seg_lengths[1, leaf]
    len_two = seg_lengths[2, mine]
    total = len_zero + len_one + len_two

    ff_cols = w_gate.shape[1]
    packed = lax.all_gather(
        jnp.concatenate([w_gate, w_up, w_down], 1), "req", axis=0, tiled=True
    )

    level_zero = node_parent[leaf_parent]
    wanted = jnp.stack([level_zero, leaf_parent], 1)
    local_slot = wanted % node_dev
    my_rows = lax.dynamic_slice_in_dim(prefix_kv, position_group * share, share, 2)
    outgoing = my_rows[jnp.arange(2)[None, :], local_slot]
    arrived = lax.all_to_all(outgoing, "req", split_axis=0, concat_axis=0, tiled=True)
    owners = wanted[mine] // node_dev
    my_part = arrived[owners, jnp.arange(2)]
    fanned = jnp.broadcast_to(my_part[None], (n_mlp,) + my_part.shape)
    levels = lax.all_to_all(fanned, ("x", "core"), split_axis=0, concat_axis=0, tiled=True)
    levels = jnp.swapaxes(levels, 0, 1).reshape(2, seg_slot, my_part.shape[-1])

    query_at = total + position_group * tok_rows + jnp.arange(tok_rows, dtype=jnp.int32)
    normed = rms_scale(tokens, attn_gain).astype(jnp.bfloat16)
    query_full = jnp.dot(normed, w_query, preferred_element_type=jnp.float32).reshape(
        tok_rows, HEADS, HD
    )
    queries = (rotate(query_full, query_at) * HD ** (-0.5)).astype(jnp.bfloat16)
    keyval_full = jnp.dot(normed, w_keyval, preferred_element_type=jnp.float32)
    new_keys = rotate(keyval_full[:, None, :HD], query_at)[:, 0].astype(jnp.bfloat16)
    new_vals = keyval_full[:, HD:].astype(jnp.bfloat16)
    new_keyval = jnp.concatenate([new_keys, new_vals], 1)
    piece = lax.all_gather(new_keyval, ("x", "core"), axis=0, tiled=True)

    seq_len = 3 * seg_slot + piece.shape[0]
    seq = jnp.zeros((seq_len, piece.shape[1]), jnp.bfloat16)
    seq = lax.dynamic_update_slice(seq, levels[0], (0, 0))
    seq = lax.dynamic_update_slice(seq, levels[1], (len_zero, 0))
    seq = lax.dynamic_update_slice(seq, own_prefix[0], (len_zero + len_one, 0))
    seq = lax.dynamic_update_slice(seq, piece, (total, 0))
    span = WINDOW + tok_rows
    first = jnp.clip(total + position_group * tok_rows - WINDOW, 0, seq_len - span)
    window = lax.dynamic_slice_in_dim(seq, first, span, 0)
    key_at = first + jnp.arange(span, dtype=jnp.int32)
    spacing = query_at[:, None] - key_at[None, :]
    allowed = ((spacing >= 0) & (spacing < WINDOW))[:, None, :]
    scores = jnp.einsum(
        "thd,kd->thk", queries, window[:, :HD], preferred_element_type=jnp.float32
    )
    top = jnp.max(jnp.where(allowed, scores, -jnp.inf), axis=-1, keepdims=True)
    weights = jnp.where(allowed, jnp.exp(scores - top), 0.0)
    denom = jnp.sum(weights, axis=-1)
    mixed = jnp.einsum(
        "thk,kd->thd",
        weights.astype(jnp.bfloat16),
        window[:, HD:],
        preferred_element_type=jnp.float32,
    )
    context = (mixed / denom[..., None]).reshape(tok_rows, HEADS * HD).astype(jnp.bfloat16)
    attn_out = jnp.dot(context, w_out, preferred_element_type=jnp.float32)
    resid = (tokens.astype(jnp.float32) + attn_out).astype(jnp.bfloat16)
    ffn_in = rms_scale(resid, ffn_gain).astype(jnp.bfloat16)
    ffn_in, packed = lax.optimization_barrier((ffn_in, packed))
    gate_full = packed[:, :ff_cols]
    up_full = packed[:, ff_cols : 2 * ff_cols]
    down_full = packed[:, 2 * ff_cols :]
    chip_rows = lax.all_gather(ffn_in, "x", axis=0, tiled=True)
    all_rows = lax.all_gather(chip_rows, "core", axis=0, tiled=True)
    gate = jnp.dot(all_rows, gate_full, preferred_element_type=jnp.float32)
    upward = jnp.dot(all_rows, up_full, preferred_element_type=jnp.float32)
    hidden = (jax.nn.gelu(gate, approximate=True) * upward).astype(jnp.bfloat16)
    partial_down = lax.dot_general(
        hidden, down_full, (((1,), (1,)), ((), ())), preferred_element_type=jnp.float32
    ).astype(jnp.bfloat16)
    pair_sum = lax.psum_scatter(partial_down, "core", scatter_dimension=0, tiled=True)
    summed = lax.psum_scatter(pair_sum, "x", scatter_dimension=0, tiled=True).astype(jnp.float32)
    return (resid.astype(jnp.float32) + summed).astype(jnp.bfloat16)


def solution(mesh):
    n_req, n_mlp = mesh.devices.shape
    fine = jax.sharding.Mesh(mesh.devices.reshape(n_req, n_mlp // 2, 2), ("req", "x", "core"))
    cols = ("x", "core")
    return jax.shard_map(
        body,
        mesh=fine,
        in_specs=(
            P(("req", "x", "core"), None),
            P(),
            P(),
            P(),
            P(),
            P(),
            P("req", cols),
            P("req", cols),
            P("req", cols),
            P(None, "req", None, None),
            P("req", None, None),
            P(),
            P(),
            P(),
        ),
        out_specs=P(("req", "x", "core"), None),
        check_vma=False,
    )
```

```python
import jax
import jax.numpy as jnp
from jax import lax
from jax.sharding import PartitionSpec as P

HEADS = 12
HD = 128
WINDOW = 1024


EPS = 1e-06


def rms_scale(values, gain):
    wide = values.astype(jnp.float32)
    return wide * lax.rsqrt(jnp.mean(wide * wide, axis=-1, keepdims=True) + EPS) * gain


def rotate(values, where_at):
    half_dim = values.shape[-1] // 2
    freqs = 10000.0 ** (-jnp.arange(half_dim, dtype=jnp.float32) / half_dim)
    angles = where_at.astype(jnp.float32)[:, None] * freqs[None, :]
    cosine = jnp.cos(angles)[:, None, :]
    sine = jnp.sin(angles)[:, None, :]
    first = values[..., :half_dim]
    second = values[..., half_dim:]
    return jnp.concatenate([first * cosine - second * sine, first * sine + second * cosine], -1)


def body(
    tokens,
    attn_gain,
    w_query,
    w_keyval,
    w_out,
    ffn_gain,
    w_gate,
    w_up,
    w_down,
    prefix_kv,
    own_prefix,
    leaf_parent,
    node_parent,
    seg_lengths,
):
    tok_rows = tokens.shape[0]
    mine = lax.axis_index("req")
    n_core = lax.axis_size("core")
    n_mlp = lax.axis_size("x") * n_core
    position_group = lax.axis_index("x") * n_core + lax.axis_index("core")
    node_dev = prefix_kv.shape[1]
    seg_slot = prefix_kv.shape[2]
    share = seg_slot // n_mlp
    leaf = leaf_parent[mine]
    upper = node_parent[leaf]
    len_zero = seg_lengths[0, upper]
    len_one = seg_lengths[1, leaf]
    len_two = seg_lengths[2, mine]
    total = len_zero + len_one + len_two

    ff_cols = w_gate.shape[1]
    packed = lax.all_gather(
        jnp.concatenate([w_gate, w_up, w_down], 1), "req", axis=0, tiled=True
    )

    level_zero = node_parent[leaf_parent]
    wanted = jnp.stack([level_zero, leaf_parent], 1)
    local_slot = wanted % node_dev
    my_rows = lax.dynamic_slice_in_dim(prefix_kv, position_group * share, share, 2)
    outgoing = my_rows[jnp.arange(2)[None, :], local_slot]
    arrived = lax.all_to_all(outgoing, "req", split_axis=0, concat_axis=0, tiled=True)
    owners = wanted[mine] // node_dev
    my_part = arrived[owners, jnp.arange(2)]
    fanned = jnp.broadcast_to(my_part[None], (n_mlp,) + my_part.shape)
    levels = lax.all_to_all(fanned, ("x", "core"), split_axis=0, concat_axis=0, tiled=True)
    levels = jnp.swapaxes(levels, 0, 1).reshape(2, seg_slot, my_part.shape[-1])

    query_at = total + position_group * tok_rows + jnp.arange(tok_rows, dtype=jnp.int32)
    normed = rms_scale(tokens, attn_gain).astype(jnp.bfloat16)
    query_full = jnp.dot(normed, w_query, preferred_element_type=jnp.float32).reshape(
        tok_rows, HEADS, HD
    )
    queries = (rotate(query_full, query_at) * HD ** (-0.5)).astype(jnp.bfloat16)
    keyval_full = jnp.dot(normed, w_keyval, preferred_element_type=jnp.float32)
    new_keys = rotate(keyval_full[:, None, :HD], query_at)[:, 0].astype(jnp.bfloat16)
    new_vals = keyval_full[:, HD:].astype(jnp.bfloat16)
    new_keyval = jnp.concatenate([new_keys, new_vals], 1)
    piece = lax.all_gather(new_keyval, ("x", "core"), axis=0, tiled=True)

    seq_len = 3 * seg_slot + piece.shape[0]
    seq = jnp.zeros((seq_len, piece.shape[1]), jnp.bfloat16)
    seq = lax.dynamic_update_slice(seq, levels[0], (0, 0))
    seq = lax.dynamic_update_slice(seq, levels[1], (len_zero, 0))
    seq = lax.dynamic_update_slice(seq, own_prefix[0], (len_zero + len_one, 0))
    seq = lax.dynamic_update_slice(seq, piece, (total, 0))
    span = WINDOW + tok_rows
    first = jnp.clip(total + position_group * tok_rows - WINDOW, 0, seq_len - span)
    window = lax.dynamic_slice_in_dim(seq, first, span, 0)
    key_at = first + jnp.arange(span, dtype=jnp.int32)
    spacing = query_at[:, None] - key_at[None, :]
    allowed = ((spacing >= 0) & (spacing < WINDOW))[:, None, :]
    scores = jnp.einsum(
        "thd,kd->thk", queries, window[:, :HD], preferred_element_type=jnp.float32
    )
    top = jnp.max(jnp.where(allowed, scores, -jnp.inf), axis=-1, keepdims=True)
    weights = jnp.where(allowed, jnp.exp(scores - top), 0.0)
    denom = jnp.sum(weights, axis=-1)
    mixed = jnp.einsum(
        "thk,kd->thd",
        weights.astype(jnp.bfloat16),
        window[:, HD:],
        preferred_element_type=jnp.float32,
    )
    context = (mixed / denom[..., None]).reshape(tok_rows, HEADS * HD).astype(jnp.bfloat16)
    attn_out = jnp.dot(context, w_out, preferred_element_type=jnp.float32)
    resid = (tokens.astype(jnp.float32) + attn_out).astype(jnp.bfloat16)
    ffn_in = rms_scale(resid, ffn_gain).astype(jnp.bfloat16)
    ffn_in, packed = lax.optimization_barrier((ffn_in, packed))
    gate_full = packed[:, :ff_cols]
    up_full = packed[:, ff_cols : 2 * ff_cols]
    down_full = packed[:, 2 * ff_cols :]
    n_chunks = 2
    chunk = tok_rows // n_chunks
    sums = []
    pending = None
    for index in range(n_chunks):
        rows = lax.all_gather(
            ffn_in[index * chunk : (index + 1) * chunk], ("x", "core"), axis=0, tiled=True
        )
        if pending is not None:
            pending, rows = lax.optimization_barrier((pending, rows))
            sums.append(lax.psum_scatter(pending, ("x", "core"), scatter_dimension=0, tiled=True))
        gate = jnp.dot(rows, gate_full, preferred_element_type=jnp.float32)
        upward = jnp.dot(rows, up_full, preferred_element_type=jnp.float32)
        hidden = (jax.nn.gelu(gate, approximate=True) * upward).astype(jnp.bfloat16)
        pending = lax.dot_general(
            hidden, down_full, (((1,), (1,)), ((), ())), preferred_element_type=jnp.float32
        ).astype(jnp.bfloat16)
    sums.append(lax.psum_scatter(pending, ("x", "core"), scatter_dimension=0, tiled=True))
    summed = jnp.concatenate(sums, 0).astype(jnp.float32)
    return (resid.astype(jnp.float32) + summed).astype(jnp.bfloat16)


def solution(mesh):
    n_req, n_mlp = mesh.devices.shape
    fine = jax.sharding.Mesh(mesh.devices.reshape(n_req, n_mlp // 2, 2), ("req", "x", "core"))
    cols = ("x", "core")
    return jax.shard_map(
        body,
        mesh=fine,
        in_specs=(
            P(("req", "x", "core"), None),
            P(),
            P(),
            P(),
            P(),
            P(),
            P("req", cols),
            P("req", cols),
            P("req", cols),
            P(None, "req", None, None),
            P("req", None, None),
            P(),
            P(),
            P(),
        ),
        out_specs=P(("req", "x", "core"), None),
        check_vma=False,
    )
```

```python
import jax
import jax.numpy as jnp
from jax import lax
from jax.sharding import PartitionSpec as P

HEADS = 12
HD = 128
WINDOW = 1024


EPS = 1e-06


def rms_scale(values, gain):
    wide = values.astype(jnp.float32)
    return wide * lax.rsqrt(jnp.mean(wide * wide, axis=-1, keepdims=True) + EPS) * gain


def rotate(values, where_at):
    half_dim = values.shape[-1] // 2
    freqs = 10000.0 ** (-jnp.arange(half_dim, dtype=jnp.float32) / half_dim)
    angles = where_at.astype(jnp.float32)[:, None] * freqs[None, :]
    cosine = jnp.cos(angles)[:, None, :]
    sine = jnp.sin(angles)[:, None, :]
    first = values[..., :half_dim]
    second = values[..., half_dim:]
    return jnp.concatenate([first * cosine - second * sine, first * sine + second * cosine], -1)


def body(
    tokens,
    attn_gain,
    w_query,
    w_keyval,
    w_out,
    ffn_gain,
    w_gate,
    w_up,
    w_down,
    prefix_kv,
    own_prefix,
    leaf_parent,
    node_parent,
    seg_lengths,
):
    tok_rows = tokens.shape[0]
    mine = lax.axis_index("req")
    n_mlp = lax.axis_size("mlp")
    position_group = lax.axis_index("mlp")
    node_dev = prefix_kv.shape[1]
    seg_slot = prefix_kv.shape[2]
    share = seg_slot // n_mlp
    leaf = leaf_parent[mine]
    upper = node_parent[leaf]
    len_zero = seg_lengths[0, upper]
    len_one = seg_lengths[1, leaf]
    len_two = seg_lengths[2, mine]
    total = len_zero + len_one + len_two

    ff_cols = w_gate.shape[1]
    packed = lax.all_gather(
        jnp.concatenate([w_gate, w_up, w_down], 1), "req", axis=0, tiled=True
    )
    gate_full = packed[:, :ff_cols]
    up_full = packed[:, ff_cols : 2 * ff_cols]
    down_full = packed[:, 2 * ff_cols :]

    level_zero = node_parent[leaf_parent]
    wanted = jnp.stack([level_zero, leaf_parent], 1)
    local_slot = wanted % node_dev
    my_rows = lax.dynamic_slice_in_dim(prefix_kv, position_group * share, share, 2)
    outgoing = my_rows[jnp.arange(2)[None, :], local_slot]
    arrived = lax.all_to_all(outgoing, "req", split_axis=0, concat_axis=0, tiled=True)
    owners = wanted[mine] // node_dev
    my_part = arrived[owners, jnp.arange(2)]
    levels = lax.all_gather(my_part, "mlp", axis=1, tiled=True)

    query_at = total + position_group * tok_rows + jnp.arange(tok_rows, dtype=jnp.int32)
    normed = rms_scale(tokens, attn_gain).astype(jnp.bfloat16)
    query_full = jnp.dot(normed, w_query, preferred_element_type=jnp.float32).reshape(
        tok_rows, HEADS, HD
    )
    queries = (rotate(query_full, query_at) * HD ** (-0.5)).astype(jnp.bfloat16)
    keyval_full = jnp.dot(normed, w_keyval, preferred_element_type=jnp.float32)
    new_keys = rotate(keyval_full[:, None, :HD], query_at)[:, 0].astype(jnp.bfloat16)
    new_vals = keyval_full[:, HD:].astype(jnp.bfloat16)
    new_keyval = jnp.concatenate([new_keys, new_vals], 1)
    back = WINDOW // tok_rows
    blocks = [
        lax.ppermute(new_keyval, "mlp", [(i, (i + shift) % n_mlp) for i in range(n_mlp)])
        for shift in range(back, 0, -1)
    ]
    new_part = jnp.concatenate(blocks + [new_keyval], 0)
    span = new_part.shape[0]

    cbuf = jnp.zeros((WINDOW + 3 * seg_slot + span, new_part.shape[1]), jnp.bfloat16)
    cbuf = lax.dynamic_update_slice(cbuf, levels[0], (WINDOW, 0))
    cbuf = lax.dynamic_update_slice(cbuf, levels[1], (WINDOW + len_zero, 0))
    cbuf = lax.dynamic_update_slice(cbuf, own_prefix[0], (WINDOW + len_zero + len_one, 0))
    cached_win = lax.dynamic_slice_in_dim(cbuf, total + position_group * tok_rows, span, 0)
    use_cached = (jnp.arange(span, dtype=jnp.int32) // tok_rows) < back - position_group
    window = jnp.where(use_cached[:, None], cached_win, new_part)
    key_at = total + position_group * tok_rows - WINDOW + jnp.arange(span, dtype=jnp.int32)
    spacing = query_at[:, None] - key_at[None, :]
    allowed = ((key_at[None, :] >= 0) & (spacing >= 0) & (spacing < WINDOW))[:, None, :]
    scores = jnp.einsum(
        "thd,kd->thk", queries, window[:, :HD], preferred_element_type=jnp.float32
    )
    top = jnp.max(jnp.where(allowed, scores, -jnp.inf), axis=-1, keepdims=True)
    weights = jnp.where(allowed, jnp.exp(scores - top), 0.0)
    denom = jnp.sum(weights, axis=-1)
    mixed = jnp.einsum(
        "thk,kd->thd",
        weights.astype(jnp.bfloat16),
        window[:, HD:],
        preferred_element_type=jnp.float32,
    )
    context = (mixed / denom[..., None]).reshape(tok_rows, HEADS * HD).astype(jnp.bfloat16)
    attn_out = jnp.dot(context, w_out, preferred_element_type=jnp.float32)
    resid = (tokens.astype(jnp.float32) + attn_out).astype(jnp.bfloat16)
    ffn_in = rms_scale(resid, ffn_gain).astype(jnp.bfloat16)
    all_rows = lax.all_gather(ffn_in, "mlp", axis=0, tiled=True)
    gate = jnp.dot(all_rows, gate_full, preferred_element_type=jnp.float32)
    upward = jnp.dot(all_rows, up_full, preferred_element_type=jnp.float32)
    hidden = (jax.nn.gelu(gate, approximate=True) * upward).astype(jnp.bfloat16)
    summed = lax.psum_scatter(
        lax.dot_general(
            hidden, down_full, (((1,), (1,)), ((), ())), preferred_element_type=jnp.float32
        ).astype(jnp.bfloat16),
        "mlp",
        scatter_dimension=0,
        tiled=True,
    ).astype(jnp.float32)
    return (resid.astype(jnp.float32) + summed).astype(jnp.bfloat16)


def solution(mesh):
    return jax.shard_map(
        body,
        mesh=mesh,
        in_specs=(
            P(("req", "mlp"), None),
            P(),
            P(),
            P(),
            P(),
            P(),
            P("req", "mlp"),
            P("req", "mlp"),
            P("req", "mlp"),
            P(None, "req", None, None),
            P("req", None, None),
            P(),
            P(),
            P(),
        ),
        out_specs=P(("req", "mlp"), None),
        check_vma=False,
    )
```

```python
import jax
import jax.numpy as jnp
from jax import lax
from jax.sharding import PartitionSpec as P

HEADS = 12
HD = 128
WINDOW = 1024


EPS = 1e-06


def rms_scale(values, gain):
    wide = values.astype(jnp.float32)
    return wide * lax.rsqrt(jnp.mean(wide * wide, axis=-1, keepdims=True) + EPS) * gain


def rotate(values, where_at):
    half_dim = values.shape[-1] // 2
    freqs = 10000.0 ** (-jnp.arange(half_dim, dtype=jnp.float32) / half_dim)
    angles = where_at.astype(jnp.float32)[:, None] * freqs[None, :]
    cosine = jnp.cos(angles)[:, None, :]
    sine = jnp.sin(angles)[:, None, :]
    first = values[..., :half_dim]
    second = values[..., half_dim:]
    return jnp.concatenate([first * cosine - second * sine, first * sine + second * cosine], -1)


def body(
    tokens,
    attn_gain,
    w_query,
    w_keyval,
    w_out,
    ffn_gain,
    w_gate,
    w_up,
    w_down,
    prefix_kv,
    own_prefix,
    leaf_parent,
    node_parent,
    seg_lengths,
):
    tok_rows = tokens.shape[0]
    mine = lax.axis_index("req")
    n_mlp = lax.axis_size("mlp")
    position_group = lax.axis_index("mlp")
    node_dev = prefix_kv.shape[1]
    seg_slot = prefix_kv.shape[2]
    share = seg_slot // n_mlp
    leaf = leaf_parent[mine]
    upper = node_parent[leaf]
    len_zero = seg_lengths[0, upper]
    len_one = seg_lengths[1, leaf]
    len_two = seg_lengths[2, mine]
    total = len_zero + len_one + len_two

    ff_cols = w_gate.shape[1]
    packed = lax.all_gather(
        jnp.concatenate([w_gate, w_up, w_down], 1), "req", axis=0, tiled=True
    )
    down_full = packed[:, 2 * ff_cols :]

    level_zero = node_parent[leaf_parent]
    wanted = jnp.stack([level_zero, leaf_parent], 1)
    local_slot = wanted % node_dev
    my_rows = lax.dynamic_slice_in_dim(prefix_kv, position_group * share, share, 2)
    outgoing = my_rows[jnp.arange(2)[None, :], local_slot]
    arrived = lax.all_to_all(outgoing, "req", split_axis=0, concat_axis=0, tiled=True)
    owners = wanted[mine] // node_dev
    my_part = arrived[owners, jnp.arange(2)]
    levels = lax.all_gather(my_part, "mlp", axis=1, tiled=True)

    query_at = total + position_group * tok_rows + jnp.arange(tok_rows, dtype=jnp.int32)
    normed = rms_scale(tokens, attn_gain).astype(jnp.bfloat16)
    query_full = jnp.dot(normed, w_query, preferred_element_type=jnp.float32).reshape(
        tok_rows, HEADS, HD
    )
    queries = (rotate(query_full, query_at) * HD ** (-0.5)).astype(jnp.bfloat16)
    keyval_full = jnp.dot(normed, w_keyval, preferred_element_type=jnp.float32)
    new_keys = rotate(keyval_full[:, None, :HD], query_at)[:, 0].astype(jnp.bfloat16)
    new_vals = keyval_full[:, HD:].astype(jnp.bfloat16)
    new_keyval = jnp.concatenate([new_keys, new_vals], 1)
    piece = lax.all_gather(new_keyval, "mlp", axis=0, tiled=True)

    sources = jnp.concatenate([levels[0], levels[1], own_prefix[0], piece], 0)
    seq_len = 3 * seg_slot + piece.shape[0]
    span = WINDOW + tok_rows
    first = jnp.clip(total + position_group * tok_rows - WINDOW, 0, seq_len - span)
    key_at = first + jnp.arange(span, dtype=jnp.int32)
    len_cut = len_zero + len_one
    source_row = jnp.where(
        key_at < len_zero,
        key_at,
        jnp.where(
            key_at < len_cut,
            key_at - len_zero + seg_slot,
            jnp.where(key_at < total, key_at - len_cut + 2 * seg_slot, key_at - total + 3 * seg_slot),
        ),
    )
    window = jnp.take(sources, source_row, axis=0, mode="clip")
    spacing = query_at[:, None] - key_at[None, :]
    allowed = ((spacing >= 0) & (spacing < WINDOW))[:, None, :]
    scores = jnp.einsum(
        "thd,kd->thk", queries, window[:, :HD], preferred_element_type=jnp.float32
    )
    top = jnp.max(jnp.where(allowed, scores, -jnp.inf), axis=-1, keepdims=True)
    weights = jnp.where(allowed, jnp.exp(scores - top), 0.0)
    denom = jnp.sum(weights, axis=-1)
    mixed = jnp.einsum(
        "thk,kd->thd",
        weights.astype(jnp.bfloat16),
        window[:, HD:],
        preferred_element_type=jnp.float32,
    )
    context = (mixed / denom[..., None]).reshape(tok_rows, HEADS * HD).astype(jnp.bfloat16)
    attn_out = jnp.dot(context, w_out, preferred_element_type=jnp.float32)
    resid = (tokens.astype(jnp.float32) + attn_out).astype(jnp.bfloat16)
    ffn_in = rms_scale(resid, ffn_gain).astype(jnp.bfloat16)
    all_rows = lax.all_gather(ffn_in, "mlp", axis=0, tiled=True)
    gate_up = jnp.dot(all_rows, packed[:, : 2 * ff_cols], preferred_element_type=jnp.float32)
    gate = gate_up[:, :ff_cols]
    upward = gate_up[:, ff_cols:]
    hidden = (jax.nn.gelu(gate, approximate=True) * upward).astype(jnp.bfloat16)
    summed = lax.psum_scatter(
        lax.dot_general(
            hidden, down_full, (((1,), (1,)), ((), ())), preferred_element_type=jnp.float32
        ).astype(jnp.bfloat16),
        "mlp",
        scatter_dimension=0,
        tiled=True,
    ).astype(jnp.float32)
    return (resid.astype(jnp.float32) + summed).astype(jnp.bfloat16)


def solution(mesh):
    return jax.shard_map(
        body,
        mesh=mesh,
        in_specs=(
            P(("req", "mlp"), None),
            P(),
            P(),
            P(),
            P(),
            P(),
            P("req", "mlp"),
            P("req", "mlp"),
            P("req", "mlp"),
            P(None, "req", None, None),
            P("req", None, None),
            P(),
            P(),
            P(),
        ),
        out_specs=P(("req", "mlp"), None),
        check_vma=False,
    )
```

```python
import jax
import jax.numpy as jnp
from jax import lax
from jax.experimental import pallas as pl
from jax.experimental.pallas import tpu as pltpu
from jax.sharding import PartitionSpec as P

HEADS = 12
HD = 128
WINDOW = 1024


EPS = 1e-06


def rms_scale(values, gain):
    wide = values.astype(jnp.float32)
    return wide * lax.rsqrt(jnp.mean(wide * wide, axis=-1, keepdims=True) + EPS) * gain


def rotate(values, where_at):
    half_dim = values.shape[-1] // 2
    freqs = 10000.0 ** (-jnp.arange(half_dim, dtype=jnp.float32) / half_dim)
    angles = where_at.astype(jnp.float32)[:, None] * freqs[None, :]
    cosine = jnp.cos(angles)[:, None, :]
    sine = jnp.sin(angles)[:, None, :]
    first = values[..., :half_dim]
    second = values[..., half_dim:]
    return jnp.concatenate([first * cosine - second * sine, first * sine + second * cosine], -1)


def _attend_kernel(where_ref, q_ref, kv_ref, o_ref):
    query = q_ref[0]
    keys = kv_ref[:, :HD]
    vals = kv_ref[:, HD:]
    scores = lax.dot_general(query, keys, (((1,), (1,)), ((), ())), preferred_element_type=jnp.float32)
    query_at = where_ref[0] + lax.broadcasted_iota(jnp.int32, scores.shape, 0)
    key_at = where_ref[1] + lax.broadcasted_iota(jnp.int32, scores.shape, 1)
    spacing = query_at - key_at
    allowed = (key_at >= 0) & (spacing >= 0) & (spacing < WINDOW)
    top = jnp.max(jnp.where(allowed, scores, -jnp.inf), axis=1, keepdims=True)
    weights = jnp.where(allowed, jnp.exp(scores - top), 0.0)
    denom = jnp.sum(weights, axis=1, keepdims=True)
    mixed = jnp.dot(weights.astype(jnp.bfloat16), vals, preferred_element_type=jnp.float32)
    o_ref[0] = (mixed / denom).astype(o_ref.dtype)

def attend_window(queries_hm, window, where):
    heads, rows, _ = queries_hm.shape
    span = window.shape[0]
    return pl.pallas_call(
        _attend_kernel,
        grid_spec=pltpu.PrefetchScalarGridSpec(
            num_scalar_prefetch=1,
            grid=(heads,),
            in_specs=[
                pl.BlockSpec((1, rows, HD), lambda h, w: (h, 0, 0)),
                pl.BlockSpec((span, 2 * HD), lambda h, w: (0, 0)),
            ],
            out_specs=pl.BlockSpec((1, rows, HD), lambda h, w: (h, 0, 0)),
        ),
        out_shape=jax.ShapeDtypeStruct((heads, rows, HD), jnp.bfloat16),
    )(where, queries_hm, window)


def body(
    tokens,
    attn_gain,
    w_query,
    w_keyval,
    w_out,
    ffn_gain,
    w_gate,
    w_up,
    w_down,
    prefix_kv,
    own_prefix,
    leaf_parent,
    node_parent,
    seg_lengths,
):
    tok_rows = tokens.shape[0]
    mine = lax.axis_index("req")
    n_mlp = lax.axis_size("mlp")
    position_group = lax.axis_index("mlp")
    node_dev = prefix_kv.shape[1]
    seg_slot = prefix_kv.shape[2]
    share = seg_slot // n_mlp
    leaf = leaf_parent[mine]
    upper = node_parent[leaf]
    len_zero = seg_lengths[0, upper]
    len_one = seg_lengths[1, leaf]
    len_two = seg_lengths[2, mine]
    total = len_zero + len_one + len_two

    ff_cols = w_gate.shape[1]
    packed = lax.all_gather(
        jnp.concatenate([w_gate, w_up, w_down], 1), "req", axis=0, tiled=True
    )
    down_full = packed[:, 2 * ff_cols :]

    level_zero = node_parent[leaf_parent]
    wanted = jnp.stack([level_zero, leaf_parent], 1)
    local_slot = wanted % node_dev
    my_rows = lax.dynamic_slice_in_dim(prefix_kv, position_group * share, share, 2)
    outgoing = my_rows[jnp.arange(2)[None, :], local_slot]
    arrived = lax.all_to_all(outgoing, "req", split_axis=0, concat_axis=0, tiled=True)
    owners = wanted[mine] // node_dev
    my_part = arrived[owners, jnp.arange(2)]
    levels = lax.all_gather(my_part, "mlp", axis=1, tiled=True)

    query_at = total + position_group * tok_rows + jnp.arange(tok_rows, dtype=jnp.int32)
    normed = rms_scale(tokens, attn_gain).astype(jnp.bfloat16)
    query_full = jnp.dot(normed, w_query, preferred_element_type=jnp.float32).reshape(
        tok_rows, HEADS, HD
    )
    queries = (rotate(query_full, query_at) * HD ** (-0.5)).astype(jnp.bfloat16)
    keyval_full = jnp.dot(normed, w_keyval, preferred_element_type=jnp.float32)
    new_keys = rotate(keyval_full[:, None, :HD], query_at)[:, 0].astype(jnp.bfloat16)
    new_vals = keyval_full[:, HD:].astype(jnp.bfloat16)
    new_keyval = jnp.concatenate([new_keys, new_vals], 1)
    piece = lax.all_gather(new_keyval, "mlp", axis=0, tiled=True)

    sources = jnp.concatenate([levels[0], levels[1], own_prefix[0], piece], 0)
    seq_len = 3 * seg_slot + piece.shape[0]
    span = WINDOW + tok_rows
    first = jnp.clip(total + position_group * tok_rows - WINDOW, 0, seq_len - span)
    key_at = first + jnp.arange(span, dtype=jnp.int32)
    len_cut = len_zero + len_one
    source_row = jnp.where(
        key_at < len_zero,
        key_at,
        jnp.where(
            key_at < len_cut,
            key_at - len_zero + seg_slot,
            jnp.where(key_at < total, key_at - len_cut + 2 * seg_slot, key_at - total + 3 * seg_slot),
        ),
    )
    window = jnp.take(sources, source_row, axis=0, mode="clip")
    where = jnp.stack([total + position_group * tok_rows, first]).astype(jnp.int32)
    heads_first = attend_window(jnp.transpose(queries, (1, 0, 2)), window, where)
    context = jnp.transpose(heads_first, (1, 0, 2)).reshape(tok_rows, HEADS * HD)
    attn_out = jnp.dot(context, w_out, preferred_element_type=jnp.float32)
    resid = (tokens.astype(jnp.float32) + attn_out).astype(jnp.bfloat16)
    ffn_in = rms_scale(resid, ffn_gain).astype(jnp.bfloat16)
    all_rows = lax.all_gather(ffn_in, "mlp", axis=0, tiled=True)
    gate_up = jnp.dot(all_rows, packed[:, : 2 * ff_cols], preferred_element_type=jnp.float32)
    gate = gate_up[:, :ff_cols]
    upward = gate_up[:, ff_cols:]
    hidden = (jax.nn.gelu(gate, approximate=True) * upward).astype(jnp.bfloat16)
    summed = lax.psum_scatter(
        lax.dot_general(
            hidden, down_full, (((1,), (1,)), ((), ())), preferred_element_type=jnp.float32
        ).astype(jnp.bfloat16),
        "mlp",
        scatter_dimension=0,
        tiled=True,
    ).astype(jnp.float32)
    return (resid.astype(jnp.float32) + summed).astype(jnp.bfloat16)


def solution(mesh):
    return jax.shard_map(
        body,
        mesh=mesh,
        in_specs=(
            P(("req", "mlp"), None),
            P(),
            P(),
            P(),
            P(),
            P(),
            P("req", "mlp"),
            P("req", "mlp"),
            P("req", "mlp"),
            P(None, "req", None, None),
            P("req", None, None),
            P(),
            P(),
            P(),
        ),
        out_specs=P(("req", "mlp"), None),
        check_vma=False,
    )
```

```python
import jax
import jax.numpy as jnp
from jax import lax
from jax.experimental import pallas as pl
from jax.experimental.pallas import tpu as pltpu
from jax.sharding import PartitionSpec as P

HEADS = 12
HD = 128
WINDOW = 1024


EPS = 1e-06


def rms_scale(values, gain):
    wide = values.astype(jnp.float32)
    return wide * lax.rsqrt(jnp.mean(wide * wide, axis=-1, keepdims=True) + EPS) * gain


def rotate(values, where_at):
    half_dim = values.shape[-1] // 2
    freqs = 10000.0 ** (-jnp.arange(half_dim, dtype=jnp.float32) / half_dim)
    angles = where_at.astype(jnp.float32)[:, None] * freqs[None, :]
    cosine = jnp.cos(angles)[:, None, :]
    sine = jnp.sin(angles)[:, None, :]
    first = values[..., :half_dim]
    second = values[..., half_dim:]
    return jnp.concatenate([first * cosine - second * sine, first * sine + second * cosine], -1)


def _attend_kernel(bias_ref, q_ref, kv_ref, o_ref):
    keys = kv_ref[:, :HD]
    vals = kv_ref[:, HD:]
    bias = bias_ref[...]
    for head in range(q_ref.shape[0]):
        scores = lax.dot_general(
            q_ref[head], keys, (((1,), (1,)), ((), ())), preferred_element_type=jnp.float32
        )
        scores = scores + bias
        top = jnp.max(scores, axis=1, keepdims=True)
        weights = jnp.exp(scores - top)
        denom = jnp.sum(weights, axis=1, keepdims=True)
        mixed = jnp.dot(weights.astype(jnp.bfloat16), vals, preferred_element_type=jnp.float32)
        o_ref[head] = (mixed / denom).astype(o_ref.dtype)


def attend_window(queries_hm, window, bias, heads_per_step=4):
    heads, rows, _ = queries_hm.shape
    span = window.shape[0]
    return pl.pallas_call(
        _attend_kernel,
        grid=(heads // heads_per_step,),
        in_specs=[
            pl.BlockSpec((rows, span), lambda h: (0, 0)),
            pl.BlockSpec((heads_per_step, rows, HD), lambda h: (h, 0, 0)),
            pl.BlockSpec((span, 2 * HD), lambda h: (0, 0)),
        ],
        out_specs=pl.BlockSpec((heads_per_step, rows, HD), lambda h: (h, 0, 0)),
        out_shape=jax.ShapeDtypeStruct((heads, rows, HD), jnp.bfloat16),
    )(bias, queries_hm, window)


def body(
    tokens,
    attn_gain,
    w_query,
    w_keyval,
    w_out,
    ffn_gain,
    w_gate,
    w_up,
    w_down,
    prefix_kv,
    own_prefix,
    leaf_parent,
    node_parent,
    seg_lengths,
):
    tok_rows = tokens.shape[0]
    mine = lax.axis_index("req")
    n_mlp = lax.axis_size("mlp")
    position_group = lax.axis_index("mlp")
    node_dev = prefix_kv.shape[1]
    seg_slot = prefix_kv.shape[2]
    share = seg_slot // n_mlp
    leaf = leaf_parent[mine]
    upper = node_parent[leaf]
    len_zero = seg_lengths[0, upper]
    len_one = seg_lengths[1, leaf]
    len_two = seg_lengths[2, mine]
    total = len_zero + len_one + len_two

    ff_cols = w_gate.shape[1]
    packed = lax.all_gather(
        jnp.concatenate([w_gate, w_up, w_down], 1), "req", axis=0, tiled=True
    )
    down_full = packed[:, 2 * ff_cols :]

    level_zero = node_parent[leaf_parent]
    wanted = jnp.stack([level_zero, leaf_parent], 1)
    local_slot = wanted % node_dev
    my_rows = lax.dynamic_slice_in_dim(prefix_kv, position_group * share, share, 2)
    outgoing = my_rows[jnp.arange(2)[None, :], local_slot]
    arrived = lax.all_to_all(outgoing, "req", split_axis=0, concat_axis=0, tiled=True)
    owners = wanted[mine] // node_dev
    my_part = arrived[owners, jnp.arange(2)]
    levels = lax.all_gather(my_part, "mlp", axis=1, tiled=True)

    query_at = total + position_group * tok_rows + jnp.arange(tok_rows, dtype=jnp.int32)
    normed = rms_scale(tokens, attn_gain).astype(jnp.bfloat16)
    query_full = jnp.dot(normed, w_query, preferred_element_type=jnp.float32).reshape(
        tok_rows, HEADS, HD
    )
    queries = (rotate(query_full, query_at) * HD ** (-0.5)).astype(jnp.bfloat16)
    keyval_full = jnp.dot(normed, w_keyval, preferred_element_type=jnp.float32)
    new_keys = rotate(keyval_full[:, None, :HD], query_at)[:, 0].astype(jnp.bfloat16)
    new_vals = keyval_full[:, HD:].astype(jnp.bfloat16)
    new_keyval = jnp.concatenate([new_keys, new_vals], 1)
    piece = lax.all_gather(new_keyval, "mlp", axis=0, tiled=True)

    sources = jnp.concatenate([levels[0], levels[1], own_prefix[0], piece], 0)
    seq_len = 3 * seg_slot + piece.shape[0]
    span = WINDOW + tok_rows
    first = jnp.clip(total + position_group * tok_rows - WINDOW, 0, seq_len - span)
    key_at = first + jnp.arange(span, dtype=jnp.int32)
    len_cut = len_zero + len_one
    source_row = jnp.where(
        key_at < len_zero,
        key_at,
        jnp.where(
            key_at < len_cut,
            key_at - len_zero + seg_slot,
            jnp.where(key_at < total, key_at - len_cut + 2 * seg_slot, key_at - total + 3 * seg_slot),
        ),
    )
    window = jnp.take(sources, source_row, axis=0, mode="clip")
    spacing = query_at[:, None] - key_at[None, :]
    allowed = (key_at[None, :] >= 0) & (spacing >= 0) & (spacing < WINDOW)
    bias = jnp.where(allowed, 0.0, -jnp.inf).astype(jnp.float32)
    heads_first = attend_window(jnp.transpose(queries, (1, 0, 2)), window, bias)
    context = jnp.transpose(heads_first, (1, 0, 2)).reshape(tok_rows, HEADS * HD)
    attn_out = jnp.dot(context, w_out, preferred_element_type=jnp.float32)
    resid = (tokens.astype(jnp.float32) + attn_out).astype(jnp.bfloat16)
    ffn_in = rms_scale(resid, ffn_gain).astype(jnp.bfloat16)
    all_rows = lax.all_gather(ffn_in, "mlp", axis=0, tiled=True)
    gate_up = jnp.dot(all_rows, packed[:, : 2 * ff_cols], preferred_element_type=jnp.float32)
    gate = gate_up[:, :ff_cols]
    upward = gate_up[:, ff_cols:]
    hidden = (jax.nn.gelu(gate, approximate=True) * upward).astype(jnp.bfloat16)
    summed = lax.psum_scatter(
        lax.dot_general(
            hidden, down_full, (((1,), (1,)), ((), ())), preferred_element_type=jnp.float32
        ).astype(jnp.bfloat16),
        "mlp",
        scatter_dimension=0,
        tiled=True,
    ).astype(jnp.float32)
    return (resid.astype(jnp.float32) + summed).astype(jnp.bfloat16)


def solution(mesh):
    return jax.shard_map(
        body,
        mesh=mesh,
        in_specs=(
            P(("req", "mlp"), None),
            P(),
            P(),
            P(),
            P(),
            P(),
            P("req", "mlp"),
            P("req", "mlp"),
            P("req", "mlp"),
            P(None, "req", None, None),
            P("req", None, None),
            P(),
            P(),
            P(),
        ),
        out_specs=P(("req", "mlp"), None),
        check_vma=False,
    )
```

```python
import jax
import jax.numpy as jnp
from jax import lax
from jax.experimental import pallas as pl
from jax.experimental.pallas import tpu as pltpu
from jax.sharding import PartitionSpec as P

HEADS = 12
HD = 128
WINDOW = 1024


EPS = 1e-06


def rms_scale(values, gain):
    wide = values.astype(jnp.float32)
    return wide * lax.rsqrt(jnp.mean(wide * wide, axis=-1, keepdims=True) + EPS) * gain


def rotate(values, where_at):
    half_dim = values.shape[-1] // 2
    freqs = 10000.0 ** (-jnp.arange(half_dim, dtype=jnp.float32) / half_dim)
    angles = where_at.astype(jnp.float32)[:, None] * freqs[None, :]
    cosine = jnp.cos(angles)[:, None, :]
    sine = jnp.sin(angles)[:, None, :]
    first = values[..., :half_dim]
    second = values[..., half_dim:]
    return jnp.concatenate([first * cosine - second * sine, first * sine + second * cosine], -1)


def _attend_kernel(bias_ref, q_ref, kv_ref, o_ref):
    keys = kv_ref[:, :HD]
    vals = kv_ref[:, HD:]
    bias = bias_ref[...]
    for head in range(q_ref.shape[0]):
        scores = lax.dot_general(
            q_ref[head], keys, (((1,), (1,)), ((), ())), preferred_element_type=jnp.float32
        )
        scores = scores + bias
        top = jnp.max(scores, axis=1, keepdims=True)
        weights = jnp.exp(scores - top)
        denom = jnp.sum(weights, axis=1, keepdims=True)
        mixed = jnp.dot(weights.astype(jnp.bfloat16), vals, preferred_element_type=jnp.float32)
        o_ref[head] = (mixed / denom).astype(o_ref.dtype)


def attend_window(queries_hm, window, bias, heads_per_step=4):
    heads, rows, _ = queries_hm.shape
    span = window.shape[0]
    return pl.pallas_call(
        _attend_kernel,
        grid=(heads // heads_per_step,),
        in_specs=[
            pl.BlockSpec((rows, span), lambda h: (0, 0)),
            pl.BlockSpec((heads_per_step, rows, HD), lambda h: (h, 0, 0)),
            pl.BlockSpec((span, 2 * HD), lambda h: (0, 0)),
        ],
        out_specs=pl.BlockSpec((heads_per_step, rows, HD), lambda h: (h, 0, 0)),
        out_shape=jax.ShapeDtypeStruct((heads, rows, HD), jnp.bfloat16),
    )(bias, queries_hm, window)


def body(
    tokens,
    attn_gain,
    w_query,
    w_keyval,
    w_out,
    ffn_gain,
    w_gate,
    w_up,
    w_down,
    prefix_kv,
    own_prefix,
    leaf_parent,
    node_parent,
    seg_lengths,
):
    tok_rows = tokens.shape[0]
    mine = lax.axis_index("req")
    n_mlp = lax.axis_size("mlp")
    position_group = lax.axis_index("mlp")
    node_dev = prefix_kv.shape[1]
    seg_slot = prefix_kv.shape[2]
    share = seg_slot // n_mlp
    leaf = leaf_parent[mine]
    upper = node_parent[leaf]
    len_zero = seg_lengths[0, upper]
    len_one = seg_lengths[1, leaf]
    len_two = seg_lengths[2, mine]
    total = len_zero + len_one + len_two

    ff_cols = w_gate.shape[1]
    packed = lax.all_gather(
        jnp.concatenate([w_gate, w_up, w_down], 1), "req", axis=0, tiled=True
    )
    down_full = packed[:, 2 * ff_cols :]

    level_zero = node_parent[leaf_parent]
    wanted = jnp.stack([level_zero, leaf_parent], 1)
    local_slot = wanted % node_dev
    my_rows = lax.dynamic_slice_in_dim(prefix_kv, position_group * share, share, 2)
    outgoing = my_rows[jnp.arange(2)[None, :], local_slot]
    arrived = lax.all_to_all(outgoing, "req", split_axis=0, concat_axis=0, tiled=True)
    owners = wanted[mine] // node_dev
    my_part = arrived[owners, jnp.arange(2)]
    levels = lax.all_gather(my_part, "mlp", axis=1, tiled=True)

    query_at = total + position_group * tok_rows + jnp.arange(tok_rows, dtype=jnp.int32)
    normed = rms_scale(tokens, attn_gain).astype(jnp.bfloat16)
    query_full = jnp.dot(normed, w_query, preferred_element_type=jnp.float32).reshape(
        tok_rows, HEADS, HD
    )
    queries = (rotate(query_full, query_at) * HD ** (-0.5)).astype(jnp.bfloat16)
    keyval_full = jnp.dot(normed, w_keyval, preferred_element_type=jnp.float32)
    new_keys = rotate(keyval_full[:, None, :HD], query_at)[:, 0].astype(jnp.bfloat16)
    new_vals = keyval_full[:, HD:].astype(jnp.bfloat16)
    new_keyval = jnp.concatenate([new_keys, new_vals], 1)
    back = WINDOW // tok_rows
    blocks = [
        lax.ppermute(new_keyval, "mlp", [(i, (i + shift) % n_mlp) for i in range(n_mlp)])
        for shift in range(back, 0, -1)
    ]
    sources = jnp.concatenate([levels[0], levels[1], own_prefix[0]] + blocks + [new_keyval], 0)
    span = (back + 1) * tok_rows
    first = total + position_group * tok_rows - WINDOW
    row = jnp.arange(span, dtype=jnp.int32)
    key_at = first + row
    len_cut = len_zero + len_one
    source_row = jnp.where(
        key_at < len_zero,
        key_at,
        jnp.where(
            key_at < len_cut,
            key_at - len_zero + seg_slot,
            jnp.where(key_at < total, key_at - len_cut + 2 * seg_slot, row + 3 * seg_slot),
        ),
    )
    window = jnp.take(sources, source_row, axis=0, mode="clip")
    spacing = query_at[:, None] - key_at[None, :]
    allowed = (key_at[None, :] >= 0) & (spacing >= 0) & (spacing < WINDOW)
    bias = jnp.where(allowed, 0.0, -jnp.inf).astype(jnp.float32)
    heads_first = attend_window(jnp.transpose(queries, (1, 0, 2)), window, bias)
    context = jnp.transpose(heads_first, (1, 0, 2)).reshape(tok_rows, HEADS * HD)
    attn_out = jnp.dot(context, w_out, preferred_element_type=jnp.float32)
    resid = (tokens.astype(jnp.float32) + attn_out).astype(jnp.bfloat16)
    ffn_in = rms_scale(resid, ffn_gain).astype(jnp.bfloat16)
    all_rows = lax.all_gather(ffn_in, "mlp", axis=0, tiled=True)
    gate_up = jnp.dot(all_rows, packed[:, : 2 * ff_cols], preferred_element_type=jnp.float32)
    gate = gate_up[:, :ff_cols]
    upward = gate_up[:, ff_cols:]
    hidden = (jax.nn.gelu(gate, approximate=True) * upward).astype(jnp.bfloat16)
    summed = lax.psum_scatter(
        lax.dot_general(
            hidden, down_full, (((1,), (1,)), ((), ())), preferred_element_type=jnp.float32
        ).astype(jnp.bfloat16),
        "mlp",
        scatter_dimension=0,
        tiled=True,
    ).astype(jnp.float32)
    return (resid.astype(jnp.float32) + summed).astype(jnp.bfloat16)


def solution(mesh):
    return jax.shard_map(
        body,
        mesh=mesh,
        in_specs=(
            P(("req", "mlp"), None),
            P(),
            P(),
            P(),
            P(),
            P(),
            P("req", "mlp"),
            P("req", "mlp"),
            P("req", "mlp"),
            P(None, "req", None, None),
            P("req", None, None),
            P(),
            P(),
            P(),
        ),
        out_specs=P(("req", "mlp"), None),
        check_vma=False,
    )
```

```python
import jax
import jax.numpy as jnp
from jax import lax
from jax.experimental import pallas as pl
from jax.experimental.pallas import tpu as pltpu
from jax.sharding import PartitionSpec as P

HEADS = 12
HD = 128
WINDOW = 1024


EPS = 1e-06


def rms_scale(values, gain):
    wide = values.astype(jnp.float32)
    return wide * lax.rsqrt(jnp.mean(wide * wide, axis=-1, keepdims=True) + EPS) * gain


def rotate(values, where_at):
    half_dim = values.shape[-1] // 2
    freqs = 10000.0 ** (-jnp.arange(half_dim, dtype=jnp.float32) / half_dim)
    angles = where_at.astype(jnp.float32)[:, None] * freqs[None, :]
    cosine = jnp.cos(angles)
    sine = jnp.sin(angles)
    cos_both = jnp.concatenate([cosine, cosine], -1)[:, None, :]
    sin_signed = jnp.concatenate([-sine, sine], -1)[:, None, :]
    swapped = jnp.concatenate([values[..., half_dim:], values[..., :half_dim]], -1)
    return values * cos_both + swapped * sin_signed


def _attend_kernel(where_ref, q_ref, kv_ref, o_ref):
    keys = kv_ref[:, :HD]
    vals = kv_ref[:, HD:]
    shape = (q_ref.shape[0], kv_ref.shape[0])
    query_at = where_ref[0] + lax.broadcasted_iota(jnp.int32, shape, 0)
    key_at = where_ref[1] + lax.broadcasted_iota(jnp.int32, shape, 1)
    spacing = query_at - key_at
    allowed = (key_at >= 0) & (spacing >= 0) & (spacing < WINDOW)
    bias = jnp.where(allowed, 0.0, -jnp.inf).astype(jnp.float32)
    for head in range(q_ref.shape[1] // HD):
        cols = pl.ds(head * HD, HD)
        scores = lax.dot_general(
            q_ref[:, cols], keys, (((1,), (1,)), ((), ())), preferred_element_type=jnp.float32
        )
        scores = scores + bias
        top = jnp.max(scores, axis=1, keepdims=True)
        weights = jnp.exp(scores - top)
        denom = jnp.sum(weights, axis=1, keepdims=True)
        mixed = jnp.dot(weights.astype(jnp.bfloat16), vals, preferred_element_type=jnp.float32)
        o_ref[:, cols] = (mixed / denom).astype(o_ref.dtype)


def attend_window(queries, window, where, heads_per_step=4):
    rows, width = queries.shape
    span = window.shape[0]
    step_cols = heads_per_step * HD
    return pl.pallas_call(
        _attend_kernel,
        grid_spec=pltpu.PrefetchScalarGridSpec(
            num_scalar_prefetch=1,
            grid=(width // step_cols,),
            in_specs=[
                pl.BlockSpec((rows, step_cols), lambda h, w: (0, h)),
                pl.BlockSpec((span, 2 * HD), lambda h, w: (0, 0)),
            ],
            out_specs=pl.BlockSpec((rows, step_cols), lambda h, w: (0, h)),
        ),
        out_shape=jax.ShapeDtypeStruct((rows, width), jnp.bfloat16),
    )(where, queries, window)


def body(
    tokens,
    attn_gain,
    w_query,
    w_keyval,
    w_out,
    ffn_gain,
    w_gate,
    w_up,
    w_down,
    prefix_kv,
    own_prefix,
    leaf_parent,
    node_parent,
    seg_lengths,
):
    tok_rows = tokens.shape[0]
    mine = lax.axis_index("req")
    n_mlp = lax.axis_size("mlp")
    position_group = lax.axis_index("mlp")
    node_dev = prefix_kv.shape[1]
    seg_slot = prefix_kv.shape[2]
    share = seg_slot // n_mlp
    leaf = leaf_parent[mine]
    upper = node_parent[leaf]
    len_zero = seg_lengths[0, upper]
    len_one = seg_lengths[1, leaf]
    len_two = seg_lengths[2, mine]
    total = len_zero + len_one + len_two

    ff_cols = w_gate.shape[1]
    packed = lax.all_gather(
        jnp.concatenate([w_gate, w_up, w_down], 1), "req", axis=0, tiled=True
    )
    down_full = packed[:, 2 * ff_cols :]

    level_zero = node_parent[leaf_parent]
    wanted = jnp.stack([level_zero, leaf_parent], 1)
    local_slot = wanted % node_dev
    my_rows = lax.dynamic_slice_in_dim(prefix_kv, position_group * share, share, 2)
    outgoing = my_rows[jnp.arange(2)[None, :], local_slot]
    arrived = lax.all_to_all(outgoing, "req", split_axis=0, concat_axis=0, tiled=True)
    owners = wanted[mine] // node_dev
    my_part = arrived[owners, jnp.arange(2)]
    levels = lax.all_gather(my_part, "mlp", axis=1, tiled=True)

    query_at = total + position_group * tok_rows + jnp.arange(tok_rows, dtype=jnp.int32)
    normed = rms_scale(tokens, attn_gain).astype(jnp.bfloat16)
    query_full = jnp.dot(normed, w_query, preferred_element_type=jnp.float32).reshape(
        tok_rows, HEADS, HD
    )
    queries = (rotate(query_full, query_at) * HD ** (-0.5)).astype(jnp.bfloat16)
    keyval_full = jnp.dot(normed, w_keyval, preferred_element_type=jnp.float32)
    new_keys = rotate(keyval_full[:, None, :HD], query_at)[:, 0].astype(jnp.bfloat16)
    new_vals = keyval_full[:, HD:].astype(jnp.bfloat16)
    new_keyval = jnp.concatenate([new_keys, new_vals], 1)
    back = WINDOW // tok_rows
    blocks = [
        lax.ppermute(new_keyval, "mlp", [(i, (i + shift) % n_mlp) for i in range(n_mlp)])
        for shift in range(back, 0, -1)
    ]
    sources = jnp.concatenate([levels[0], levels[1], own_prefix[0]] + blocks + [new_keyval], 0)
    span = (back + 1) * tok_rows
    first = total + position_group * tok_rows - WINDOW
    row = jnp.arange(span, dtype=jnp.int32)
    key_at = first + row
    len_cut = len_zero + len_one
    source_row = jnp.where(
        key_at < len_zero,
        key_at,
        jnp.where(
            key_at < len_cut,
            key_at - len_zero + seg_slot,
            jnp.where(key_at < total, key_at - len_cut + 2 * seg_slot, row + 3 * seg_slot),
        ),
    )
    window = jnp.take(sources, source_row, axis=0, mode="clip")
    where = jnp.stack([total + position_group * tok_rows, first]).astype(jnp.int32)
    context = attend_window(queries.reshape(tok_rows, HEADS * HD), window, where)
    attn_out = jnp.dot(context, w_out, preferred_element_type=jnp.float32)
    resid = (tokens.astype(jnp.float32) + attn_out).astype(jnp.bfloat16)
    ffn_in = rms_scale(resid, ffn_gain).astype(jnp.bfloat16)
    all_rows = lax.all_gather(ffn_in, "mlp", axis=0, tiled=True)
    gate_up = jnp.dot(all_rows, packed[:, : 2 * ff_cols], preferred_element_type=jnp.float32)
    gate = gate_up[:, :ff_cols]
    upward = gate_up[:, ff_cols:]
    hidden = (jax.nn.gelu(gate, approximate=True) * upward).astype(jnp.bfloat16)
    summed = lax.psum_scatter(
        lax.dot_general(
            hidden, down_full, (((1,), (1,)), ((), ())), preferred_element_type=jnp.float32
        ).astype(jnp.bfloat16),
        "mlp",
        scatter_dimension=0,
        tiled=True,
    ).astype(jnp.float32)
    return (resid.astype(jnp.float32) + summed).astype(jnp.bfloat16)


def solution(mesh):
    return jax.shard_map(
        body,
        mesh=mesh,
        in_specs=(
            P(("req", "mlp"), None),
            P(),
            P(),
            P(),
            P(),
            P(),
            P("req", "mlp"),
            P("req", "mlp"),
            P("req", "mlp"),
            P(None, "req", None, None),
            P("req", None, None),
            P(),
            P(),
            P(),
        ),
        out_specs=P(("req", "mlp"), None),
        check_vma=False,
    )
```

```python
import jax
import jax.numpy as jnp
from jax import lax
from jax.experimental import pallas as pl
from jax.experimental.pallas import tpu as pltpu
from jax.sharding import PartitionSpec as P

HEADS = 12
HD = 128
WINDOW = 1024


EPS = 1e-06


def rms_scale(values, gain):
    wide = values.astype(jnp.float32)
    return wide * lax.rsqrt(jnp.mean(wide * wide, axis=-1, keepdims=True) + EPS) * gain


def rotate(values, where_at):
    half_dim = values.shape[-1] // 2
    freqs = 10000.0 ** (-jnp.arange(half_dim, dtype=jnp.float32) / half_dim)
    angles = where_at.astype(jnp.float32)[:, None] * freqs[None, :]
    cosine = jnp.cos(angles)
    sine = jnp.sin(angles)
    cos_both = jnp.concatenate([cosine, cosine], -1)[:, None, :]
    sin_signed = jnp.concatenate([-sine, sine], -1)[:, None, :]
    swapped = jnp.concatenate([values[..., half_dim:], values[..., :half_dim]], -1)
    return values * cos_both + swapped * sin_signed


def _attend_kernel(where_ref, q_ref, kv_ref, o_ref):
    keys = kv_ref[:, :HD]
    vals = kv_ref[:, HD:]
    shape = (q_ref.shape[0], kv_ref.shape[0])
    query_at = where_ref[0] + lax.broadcasted_iota(jnp.int32, shape, 0)
    key_at = where_ref[1] + lax.broadcasted_iota(jnp.int32, shape, 1)
    spacing = query_at - key_at
    allowed = (key_at >= 0) & (spacing >= 0) & (spacing < WINDOW)
    bias = jnp.where(allowed, 0.0, -jnp.inf).astype(jnp.float32)
    for head in range(q_ref.shape[1] // HD):
        cols = pl.ds(head * HD, HD)
        scores = lax.dot_general(
            q_ref[:, cols], keys, (((1,), (1,)), ((), ())), preferred_element_type=jnp.float32
        )
        scores = scores + bias
        top = jnp.max(scores, axis=1, keepdims=True)
        weights = jnp.exp(scores - top)
        denom = jnp.sum(weights, axis=1, keepdims=True)
        mixed = jnp.dot(weights.astype(jnp.bfloat16), vals, preferred_element_type=jnp.float32)
        o_ref[:, cols] = (mixed / denom).astype(o_ref.dtype)


def attend_window(queries, window, where, heads_per_step=4):
    rows, width = queries.shape
    span = window.shape[0]
    step_cols = heads_per_step * HD
    return pl.pallas_call(
        _attend_kernel,
        grid_spec=pltpu.PrefetchScalarGridSpec(
            num_scalar_prefetch=1,
            grid=(width // step_cols,),
            in_specs=[
                pl.BlockSpec((rows, step_cols), lambda h, w: (0, h)),
                pl.BlockSpec((span, 2 * HD), lambda h, w: (0, 0)),
            ],
            out_specs=pl.BlockSpec((rows, step_cols), lambda h, w: (0, h)),
        ),
        out_shape=jax.ShapeDtypeStruct((rows, width), jnp.bfloat16),
    )(where, queries, window)


def _ffn_kernel(x_ref, w_ref, o_ref):
    rows = x_ref[...]
    width = w_ref.shape[1] // 3
    gate = jnp.dot(rows, w_ref[:, :width], preferred_element_type=jnp.float32)
    upward = jnp.dot(rows, w_ref[:, width : 2 * width], preferred_element_type=jnp.float32)
    hidden = (jax.nn.gelu(gate, approximate=True) * upward).astype(jnp.bfloat16)
    partial_down = lax.dot_general(
        hidden, w_ref[:, 2 * width :], (((1,), (1,)), ((), ())), preferred_element_type=jnp.float32
    )
    o_ref[...] = partial_down.astype(o_ref.dtype)


def ffn_block(all_rows, packed, block_rows=512):
    rows, model = all_rows.shape
    return pl.pallas_call(
        _ffn_kernel,
        grid=(rows // block_rows,),
        in_specs=[
            pl.BlockSpec((block_rows, model), lambda i: (i, 0)),
            pl.BlockSpec(packed.shape, lambda i: (0, 0)),
        ],
        out_specs=pl.BlockSpec((block_rows, model), lambda i: (i, 0)),
        out_shape=jax.ShapeDtypeStruct((rows, model), jnp.bfloat16),
    )(all_rows, packed)


def body(
    tokens,
    attn_gain,
    w_query,
    w_keyval,
    w_out,
    ffn_gain,
    w_gate,
    w_up,
    w_down,
    prefix_kv,
    own_prefix,
    leaf_parent,
    node_parent,
    seg_lengths,
):
    tok_rows = tokens.shape[0]
    mine = lax.axis_index("req")
    n_mlp = lax.axis_size("mlp")
    position_group = lax.axis_index("mlp")
    node_dev = prefix_kv.shape[1]
    seg_slot = prefix_kv.shape[2]
    share = seg_slot // n_mlp
    leaf = leaf_parent[mine]
    upper = node_parent[leaf]
    len_zero = seg_lengths[0, upper]
    len_one = seg_lengths[1, leaf]
    len_two = seg_lengths[2, mine]
    total = len_zero + len_one + len_two

    ff_cols = w_gate.shape[1]
    lanes = -(-ff_cols // 128) * 128
    padded = [jnp.pad(part, ((0, 0), (0, lanes - ff_cols))) for part in (w_gate, w_up, w_down)]
    packed = lax.all_gather(jnp.concatenate(padded, 1), "req", axis=0, tiled=True)

    level_zero = node_parent[leaf_parent]
    wanted = jnp.stack([level_zero, leaf_parent], 1)
    local_slot = wanted % node_dev
    my_rows = lax.dynamic_slice_in_dim(prefix_kv, position_group * share, share, 2)
    outgoing = my_rows[jnp.arange(2)[None, :], local_slot]
    arrived = lax.all_to_all(outgoing, "req", split_axis=0, concat_axis=0, tiled=True)
    owners = wanted[mine] // node_dev
    my_part = arrived[owners, jnp.arange(2)]
    levels = lax.all_gather(my_part, "mlp", axis=1, tiled=True)

    query_at = total + position_group * tok_rows + jnp.arange(tok_rows, dtype=jnp.int32)
    normed = rms_scale(tokens, attn_gain).astype(jnp.bfloat16)
    query_full = jnp.dot(normed, w_query, preferred_element_type=jnp.float32).reshape(
        tok_rows, HEADS, HD
    )
    queries = (rotate(query_full, query_at) * HD ** (-0.5)).astype(jnp.bfloat16)
    keyval_full = jnp.dot(normed, w_keyval, preferred_element_type=jnp.float32)
    new_keys = rotate(keyval_full[:, None, :HD], query_at)[:, 0].astype(jnp.bfloat16)
    new_vals = keyval_full[:, HD:].astype(jnp.bfloat16)
    new_keyval = jnp.concatenate([new_keys, new_vals], 1)
    back = WINDOW // tok_rows
    blocks = [
        lax.ppermute(new_keyval, "mlp", [(i, (i + shift) % n_mlp) for i in range(n_mlp)])
        for shift in range(back, 0, -1)
    ]
    sources = jnp.concatenate([levels[0], levels[1], own_prefix[0]] + blocks + [new_keyval], 0)
    span = (back + 1) * tok_rows
    first = total + position_group * tok_rows - WINDOW
    row = jnp.arange(span, dtype=jnp.int32)
    key_at = first + row
    len_cut = len_zero + len_one
    source_row = jnp.where(
        key_at < len_zero,
        key_at,
        jnp.where(
            key_at < len_cut,
            key_at - len_zero + seg_slot,
            jnp.where(key_at < total, key_at - len_cut + 2 * seg_slot, row + 3 * seg_slot),
        ),
    )
    window = jnp.take(sources, source_row, axis=0, mode="clip")
    where = jnp.stack([total + position_group * tok_rows, first]).astype(jnp.int32)
    context = attend_window(queries.reshape(tok_rows, HEADS * HD), window, where)
    attn_out = jnp.dot(context, w_out, preferred_element_type=jnp.float32)
    resid = (tokens.astype(jnp.float32) + attn_out).astype(jnp.bfloat16)
    ffn_in = rms_scale(resid, ffn_gain).astype(jnp.bfloat16)
    all_rows = lax.all_gather(ffn_in, "mlp", axis=0, tiled=True)
    partial_down = ffn_block(all_rows, packed)
    summed = lax.psum_scatter(
        partial_down, "mlp", scatter_dimension=0, tiled=True
    ).astype(jnp.float32)
    return (resid.astype(jnp.float32) + summed).astype(jnp.bfloat16)


def solution(mesh):
    return jax.shard_map(
        body,
        mesh=mesh,
        in_specs=(
            P(("req", "mlp"), None),
            P(),
            P(),
            P(),
            P(),
            P(),
            P("req", "mlp"),
            P("req", "mlp"),
            P("req", "mlp"),
            P(None, "req", None, None),
            P("req", None, None),
            P(),
            P(),
            P(),
        ),
        out_specs=P(("req", "mlp"), None),
        check_vma=False,
    )
```

```python
import jax
import jax.numpy as jnp
from jax import lax
from jax.experimental import pallas as pl
from jax.experimental.pallas import tpu as pltpu
from jax.sharding import PartitionSpec as P

HEADS = 12
HD = 128
WINDOW = 1024


EPS = 1e-06


def rms_scale(values, gain):
    wide = values.astype(jnp.float32)
    return wide * lax.rsqrt(jnp.mean(wide * wide, axis=-1, keepdims=True) + EPS) * gain


def rotate(values, where_at):
    half_dim = values.shape[-1] // 2
    freqs = 10000.0 ** (-jnp.arange(half_dim, dtype=jnp.float32) / half_dim)
    angles = where_at.astype(jnp.float32)[:, None] * freqs[None, :]
    cosine = jnp.cos(angles)
    sine = jnp.sin(angles)
    cos_both = jnp.concatenate([cosine, cosine], -1)[:, None, :]
    sin_signed = jnp.concatenate([-sine, sine], -1)[:, None, :]
    swapped = jnp.concatenate([values[..., half_dim:], values[..., :half_dim]], -1)
    return values * cos_both + swapped * sin_signed


def _attend_kernel(where_ref, q_ref, kv_ref, o_ref):
    keys = kv_ref[:, :HD]
    vals = kv_ref[:, HD:]
    shape = (q_ref.shape[0], kv_ref.shape[0])
    query_at = where_ref[0] + lax.broadcasted_iota(jnp.int32, shape, 0)
    key_at = where_ref[1] + lax.broadcasted_iota(jnp.int32, shape, 1)
    spacing = query_at - key_at
    allowed = (key_at >= 0) & (spacing >= 0) & (spacing < WINDOW)
    bias = jnp.where(allowed, 0.0, -jnp.inf).astype(jnp.float32)
    for head in range(q_ref.shape[1] // HD):
        cols = pl.ds(head * HD, HD)
        scores = lax.dot_general(
            q_ref[:, cols], keys, (((1,), (1,)), ((), ())), preferred_element_type=jnp.float32
        )
        scores = scores + bias
        top = jnp.max(scores, axis=1, keepdims=True)
        weights = jnp.exp(scores - top)
        denom = jnp.sum(weights, axis=1, keepdims=True)
        mixed = jnp.dot(weights.astype(jnp.bfloat16), vals, preferred_element_type=jnp.float32)
        o_ref[:, cols] = (mixed / denom).astype(o_ref.dtype)


def attend_window(queries, window, where, heads_per_step=4):
    rows, width = queries.shape
    span = window.shape[0]
    step_cols = heads_per_step * HD
    return pl.pallas_call(
        _attend_kernel,
        grid_spec=pltpu.PrefetchScalarGridSpec(
            num_scalar_prefetch=1,
            grid=(width // step_cols,),
            in_specs=[
                pl.BlockSpec((rows, step_cols), lambda h, w: (0, h)),
                pl.BlockSpec((span, 2 * HD), lambda h, w: (0, 0)),
            ],
            out_specs=pl.BlockSpec((rows, step_cols), lambda h, w: (0, h)),
        ),
        out_shape=jax.ShapeDtypeStruct((rows, width), jnp.bfloat16),
    )(where, queries, window)


def body(
    tokens,
    attn_gain,
    w_query,
    w_keyval,
    w_out,
    ffn_gain,
    w_gate,
    w_up,
    w_down,
    prefix_kv,
    own_prefix,
    leaf_parent,
    node_parent,
    seg_lengths,
):
    tok_rows = tokens.shape[0]
    mine = lax.axis_index("req")
    n_mlp = lax.axis_size("mlp")
    position_group = lax.axis_index("mlp")
    node_dev = prefix_kv.shape[1]
    seg_slot = prefix_kv.shape[2]
    share = seg_slot // n_mlp
    level_zero = node_parent[leaf_parent]
    n_requests = leaf_parent.shape[0]
    all_lengths = jnp.stack(
        [seg_lengths[0][level_zero], seg_lengths[1][leaf_parent], seg_lengths[2, :n_requests]]
    )
    my_lengths = lax.dynamic_index_in_dim(all_lengths, mine, 1, keepdims=False)
    len_zero = my_lengths[0]
    len_one = my_lengths[1]
    total = len_zero + len_one + my_lengths[2]

    ff_cols = w_gate.shape[1]
    packed = lax.all_gather(
        jnp.concatenate([w_gate, w_up, w_down], 1), "req", axis=0, tiled=True
    )
    down_full = packed[:, 2 * ff_cols :]

    wanted = jnp.stack([level_zero, leaf_parent], 1)
    local_slot = wanted % node_dev
    my_rows = lax.dynamic_slice_in_dim(prefix_kv, position_group * share, share, 2)
    outgoing = my_rows[jnp.arange(2)[None, :], local_slot]
    arrived = lax.all_to_all(outgoing, "req", split_axis=0, concat_axis=0, tiled=True)
    owners = wanted[mine] // node_dev
    my_part = arrived[owners, jnp.arange(2)]
    levels = lax.all_gather(my_part, "mlp", axis=1, tiled=True)

    query_at = total + position_group * tok_rows + jnp.arange(tok_rows, dtype=jnp.int32)
    normed = rms_scale(tokens, attn_gain).astype(jnp.bfloat16)
    query_full = jnp.dot(normed, w_query, preferred_element_type=jnp.float32).reshape(
        tok_rows, HEADS, HD
    )
    queries = (rotate(query_full, query_at) * HD ** (-0.5)).astype(jnp.bfloat16)
    keyval_full = jnp.dot(normed, w_keyval, preferred_element_type=jnp.float32)
    new_keys = rotate(keyval_full[:, None, :HD], query_at)[:, 0].astype(jnp.bfloat16)
    new_vals = keyval_full[:, HD:].astype(jnp.bfloat16)
    new_keyval = jnp.concatenate([new_keys, new_vals], 1)
    back = WINDOW // tok_rows
    blocks = [
        lax.ppermute(new_keyval, "mlp", [(i, (i + shift) % n_mlp) for i in range(n_mlp)])
        for shift in range(back, 0, -1)
    ]
    sources = jnp.concatenate([levels[0], levels[1], own_prefix[0]] + blocks + [new_keyval], 0)
    span = (back + 1) * tok_rows
    first = total + position_group * tok_rows - WINDOW
    row = jnp.arange(span, dtype=jnp.int32)
    key_at = first + row
    len_cut = len_zero + len_one
    source_row = jnp.where(
        key_at < len_zero,
        key_at,
        jnp.where(
            key_at < len_cut,
            key_at - len_zero + seg_slot,
            jnp.where(key_at < total, key_at - len_cut + 2 * seg_slot, row + 3 * seg_slot),
        ),
    )
    window = jnp.take(sources, source_row, axis=0, mode="clip")
    where = jnp.stack([total + position_group * tok_rows, first]).astype(jnp.int32)
    context = attend_window(queries.reshape(tok_rows, HEADS * HD), window, where)
    attn_out = jnp.dot(context, w_out, preferred_element_type=jnp.float32)
    resid = (tokens.astype(jnp.float32) + attn_out).astype(jnp.bfloat16)
    ffn_in = rms_scale(resid, ffn_gain).astype(jnp.bfloat16)
    all_rows = lax.all_gather(ffn_in, "mlp", axis=0, tiled=True)
    gate_up = jnp.dot(all_rows, packed[:, : 2 * ff_cols], preferred_element_type=jnp.float32)
    gate = gate_up[:, :ff_cols]
    upward = gate_up[:, ff_cols:]
    hidden = (jax.nn.gelu(gate, approximate=True) * upward).astype(jnp.bfloat16)
    summed = lax.psum_scatter(
        lax.dot_general(
            hidden, down_full, (((1,), (1,)), ((), ())), preferred_element_type=jnp.float32
        ).astype(jnp.bfloat16),
        "mlp",
        scatter_dimension=0,
        tiled=True,
    ).astype(jnp.float32)
    return (resid.astype(jnp.float32) + summed).astype(jnp.bfloat16)


def solution(mesh):
    return jax.shard_map(
        body,
        mesh=mesh,
        in_specs=(
            P(("req", "mlp"), None),
            P(),
            P(),
            P(),
            P(),
            P(),
            P("req", "mlp"),
            P("req", "mlp"),
            P("req", "mlp"),
            P(None, "req", None, None),
            P("req", None, None),
            P(),
            P(),
            P(),
        ),
        out_specs=P(("req", "mlp"), None),
        check_vma=False,
    )
```

```python
import jax
import jax.numpy as jnp
from jax import lax
from jax.experimental import pallas as pl
from jax.experimental.pallas import tpu as pltpu
from jax.sharding import PartitionSpec as P

HEADS = 12
HD = 128
WINDOW = 1024


EPS = 1e-06


def rms_scale(values, gain):
    wide = values.astype(jnp.float32)
    return wide * lax.rsqrt(jnp.mean(wide * wide, axis=-1, keepdims=True) + EPS) * gain


def rotate(values, where_at):
    half_dim = values.shape[-1] // 2
    freqs = 10000.0 ** (-jnp.arange(half_dim, dtype=jnp.float32) / half_dim)
    angles = where_at.astype(jnp.float32)[:, None] * freqs[None, :]
    cosine = jnp.cos(angles)
    sine = jnp.sin(angles)
    cos_both = jnp.concatenate([cosine, cosine], -1)[:, None, :]
    sin_signed = jnp.concatenate([-sine, sine], -1)[:, None, :]
    swapped = jnp.concatenate([values[..., half_dim:], values[..., :half_dim]], -1)
    return values * cos_both + swapped * sin_signed


def _attend_kernel(where_ref, q_ref, cos_ref, sin_ref, kv_ref, o_ref):
    keys = kv_ref[:, :HD]
    vals = kv_ref[:, HD:]
    cosine = cos_ref[...]
    sine = sin_ref[...]
    shape = (q_ref.shape[0], kv_ref.shape[0])
    query_at = where_ref[0] + lax.broadcasted_iota(jnp.int32, shape, 0)
    key_at = where_ref[1] + lax.broadcasted_iota(jnp.int32, shape, 1)
    spacing = query_at - key_at
    allowed = (key_at >= 0) & (spacing >= 0) & (spacing < WINDOW)
    bias = jnp.where(allowed, 0.0, -jnp.inf).astype(jnp.float32)
    for head in range(q_ref.shape[1] // HD):
        cols = pl.ds(head * HD, HD)
        raw = q_ref[:, cols]
        turned = raw * cosine + pltpu.roll(raw, HD // 2, 1) * sine
        query = (turned * HD ** (-0.5)).astype(jnp.bfloat16)
        scores = lax.dot_general(
            query, keys, (((1,), (1,)), ((), ())), preferred_element_type=jnp.float32
        )
        scores = scores + bias
        top = jnp.max(scores, axis=1, keepdims=True)
        weights = jnp.exp(scores - top)
        denom = jnp.sum(weights, axis=1, keepdims=True)
        mixed = jnp.dot(weights.astype(jnp.bfloat16), vals, preferred_element_type=jnp.float32)
        o_ref[:, cols] = (mixed / denom).astype(o_ref.dtype)


def attend_window(query_full, cosine, sine, window, where, heads_per_step=4):
    rows, width = query_full.shape
    span = window.shape[0]
    step_cols = heads_per_step * HD
    return pl.pallas_call(
        _attend_kernel,
        grid_spec=pltpu.PrefetchScalarGridSpec(
            num_scalar_prefetch=1,
            grid=(width // step_cols,),
            in_specs=[
                pl.BlockSpec((rows, step_cols), lambda h, w: (0, h)),
                pl.BlockSpec((rows, HD), lambda h, w: (0, 0)),
                pl.BlockSpec((rows, HD), lambda h, w: (0, 0)),
                pl.BlockSpec((span, 2 * HD), lambda h, w: (0, 0)),
            ],
            out_specs=pl.BlockSpec((rows, step_cols), lambda h, w: (0, h)),
        ),
        out_shape=jax.ShapeDtypeStruct((rows, width), jnp.bfloat16),
    )(where, query_full, cosine, sine, window)


def body(
    tokens,
    attn_gain,
    w_query,
    w_keyval,
    w_out,
    ffn_gain,
    w_gate,
    w_up,
    w_down,
    prefix_kv,
    own_prefix,
    leaf_parent,
    node_parent,
    seg_lengths,
):
    tok_rows = tokens.shape[0]
    mine = lax.axis_index("req")
    n_mlp = lax.axis_size("mlp")
    position_group = lax.axis_index("mlp")
    node_dev = prefix_kv.shape[1]
    seg_slot = prefix_kv.shape[2]
    share = seg_slot // n_mlp
    level_zero = node_parent[leaf_parent]
    n_requests = leaf_parent.shape[0]
    all_lengths = jnp.stack(
        [seg_lengths[0][level_zero], seg_lengths[1][leaf_parent], seg_lengths[2, :n_requests]]
    )
    my_lengths = lax.dynamic_index_in_dim(all_lengths, mine, 1, keepdims=False)
    len_zero = my_lengths[0]
    len_one = my_lengths[1]
    total = len_zero + len_one + my_lengths[2]

    ff_cols = w_gate.shape[1]
    packed = lax.all_gather(
        jnp.concatenate([w_gate, w_up, w_down], 1), "req", axis=0, tiled=True
    )
    down_full = packed[:, 2 * ff_cols :]

    wanted = jnp.stack([level_zero, leaf_parent], 1)
    local_slot = wanted % node_dev
    my_rows = lax.dynamic_slice_in_dim(prefix_kv, position_group * share, share, 2)
    outgoing = my_rows[jnp.arange(2)[None, :], local_slot]
    arrived = lax.all_to_all(outgoing, "req", split_axis=0, concat_axis=0, tiled=True)
    owners = wanted[mine] // node_dev
    my_part = arrived[owners, jnp.arange(2)]
    levels = lax.all_gather(my_part, "mlp", axis=1, tiled=True)

    query_at = total + position_group * tok_rows + jnp.arange(tok_rows, dtype=jnp.int32)
    normed = rms_scale(tokens, attn_gain).astype(jnp.bfloat16)
    query_full = jnp.dot(normed, w_query, preferred_element_type=jnp.float32)
    keyval_full = jnp.dot(normed, w_keyval, preferred_element_type=jnp.float32)
    half_dim = HD // 2
    freqs = 10000.0 ** (-jnp.arange(half_dim, dtype=jnp.float32) / half_dim)
    angles = query_at.astype(jnp.float32)[:, None] * jnp.concatenate([freqs, freqs])[None, :]
    cosine = jnp.cos(angles)
    sine = jnp.sin(angles) * jnp.where(jnp.arange(HD) < half_dim, -1.0, 1.0)
    raw_keys = keyval_full[:, :HD]
    swapped = jnp.concatenate([raw_keys[:, half_dim:], raw_keys[:, :half_dim]], 1)
    new_keys = (raw_keys * cosine + swapped * sine).astype(jnp.bfloat16)
    new_vals = keyval_full[:, HD:].astype(jnp.bfloat16)
    new_keyval = jnp.concatenate([new_keys, new_vals], 1)
    back = WINDOW // tok_rows
    blocks = [
        lax.ppermute(new_keyval, "mlp", [(i, (i + shift) % n_mlp) for i in range(n_mlp)])
        for shift in range(back, 0, -1)
    ]
    sources = jnp.concatenate([levels[0], levels[1], own_prefix[0]] + blocks + [new_keyval], 0)
    span = (back + 1) * tok_rows
    first = total + position_group * tok_rows - WINDOW
    row = jnp.arange(span, dtype=jnp.int32)
    key_at = first + row
    len_cut = len_zero + len_one
    source_row = jnp.where(
        key_at < len_zero,
        key_at,
        jnp.where(
            key_at < len_cut,
            key_at - len_zero + seg_slot,
            jnp.where(key_at < total, key_at - len_cut + 2 * seg_slot, row + 3 * seg_slot),
        ),
    )
    window = jnp.take(sources, source_row, axis=0, mode="clip")
    where = jnp.stack([total + position_group * tok_rows, first]).astype(jnp.int32)
    context = attend_window(query_full, cosine, sine, window, where)
    attn_out = jnp.dot(context, w_out, preferred_element_type=jnp.float32)
    resid = (tokens.astype(jnp.float32) + attn_out).astype(jnp.bfloat16)
    ffn_in = rms_scale(resid, ffn_gain).astype(jnp.bfloat16)
    all_rows = lax.all_gather(ffn_in, "mlp", axis=0, tiled=True)
    gate_up = jnp.dot(all_rows, packed[:, : 2 * ff_cols], preferred_element_type=jnp.float32)
    gate = gate_up[:, :ff_cols]
    upward = gate_up[:, ff_cols:]
    hidden = (jax.nn.gelu(gate, approximate=True) * upward).astype(jnp.bfloat16)
    summed = lax.psum_scatter(
        lax.dot_general(
            hidden, down_full, (((1,), (1,)), ((), ())), preferred_element_type=jnp.float32
        ).astype(jnp.bfloat16),
        "mlp",
        scatter_dimension=0,
        tiled=True,
    ).astype(jnp.float32)
    return (resid.astype(jnp.float32) + summed).astype(jnp.bfloat16)


def solution(mesh):
    return jax.shard_map(
        body,
        mesh=mesh,
        in_specs=(
            P(("req", "mlp"), None),
            P(),
            P(),
            P(),
            P(),
            P(),
            P("req", "mlp"),
            P("req", "mlp"),
            P("req", "mlp"),
            P(None, "req", None, None),
            P("req", None, None),
            P(),
            P(),
            P(),
        ),
        out_specs=P(("req", "mlp"), None),
        check_vma=False,
    )
```

```python
import jax
import jax.numpy as jnp
from jax import lax
from jax.experimental import pallas as pl
from jax.experimental.pallas import tpu as pltpu
from jax.sharding import PartitionSpec as P

HEADS = 12
HD = 128
WINDOW = 1024


EPS = 1e-06


def rms_scale(values, gain):
    wide = values.astype(jnp.float32)
    return wide * lax.rsqrt(jnp.mean(wide * wide, axis=-1, keepdims=True) + EPS) * gain


def rotate(values, where_at):
    half_dim = values.shape[-1] // 2
    freqs = 10000.0 ** (-jnp.arange(half_dim, dtype=jnp.float32) / half_dim)
    angles = where_at.astype(jnp.float32)[:, None] * freqs[None, :]
    cosine = jnp.cos(angles)
    sine = jnp.sin(angles)
    cos_both = jnp.concatenate([cosine, cosine], -1)[:, None, :]
    sin_signed = jnp.concatenate([-sine, sine], -1)[:, None, :]
    swapped = jnp.concatenate([values[..., half_dim:], values[..., :half_dim]], -1)
    return values * cos_both + swapped * sin_signed


def _attend_kernel(where_ref, q_ref, cos_ref, sin_ref, kv_ref, o_ref):
    keys = kv_ref[:, :HD]
    vals = kv_ref[:, HD:]
    cosine = cos_ref[...]
    sine = sin_ref[...]
    shape = (q_ref.shape[0], kv_ref.shape[0])
    query_at = where_ref[0] + lax.broadcasted_iota(jnp.int32, shape, 0)
    key_at = where_ref[1] + lax.broadcasted_iota(jnp.int32, shape, 1)
    spacing = query_at - key_at
    allowed = (key_at >= 0) & (spacing >= 0) & (spacing < WINDOW)
    bias = jnp.where(allowed, 0.0, -jnp.inf).astype(jnp.float32)
    for head in range(q_ref.shape[1] // HD):
        cols = pl.ds(head * HD, HD)
        raw = q_ref[:, cols]
        turned = raw * cosine + pltpu.roll(raw, HD // 2, 1) * sine
        query = (turned * HD ** (-0.5)).astype(jnp.bfloat16)
        scores = lax.dot_general(
            query, keys, (((1,), (1,)), ((), ())), preferred_element_type=jnp.float32
        )
        scores = scores + bias
        top = jnp.max(scores, axis=1, keepdims=True)
        weights = jnp.exp(scores - top)
        denom = jnp.sum(weights, axis=1, keepdims=True)
        mixed = jnp.dot(weights.astype(jnp.bfloat16), vals, preferred_element_type=jnp.float32)
        o_ref[:, cols] = (mixed / denom).astype(o_ref.dtype)


def attend_window(query_full, cosine, sine, window, where, heads_per_step=4):
    rows, width = query_full.shape
    span = window.shape[0]
    step_cols = heads_per_step * HD
    return pl.pallas_call(
        _attend_kernel,
        grid_spec=pltpu.PrefetchScalarGridSpec(
            num_scalar_prefetch=1,
            grid=(width // step_cols,),
            in_specs=[
                pl.BlockSpec((rows, step_cols), lambda h, w: (0, h)),
                pl.BlockSpec((rows, HD), lambda h, w: (0, 0)),
                pl.BlockSpec((rows, HD), lambda h, w: (0, 0)),
                pl.BlockSpec((span, 2 * HD), lambda h, w: (0, 0)),
            ],
            out_specs=pl.BlockSpec((rows, step_cols), lambda h, w: (0, h)),
        ),
        out_shape=jax.ShapeDtypeStruct((rows, width), jnp.bfloat16),
    )(where, query_full, cosine, sine, window)


def body(
    tokens,
    attn_gain,
    w_query,
    w_keyval,
    w_out,
    ffn_gain,
    w_gate,
    w_up,
    w_down,
    prefix_kv,
    own_prefix,
    leaf_parent,
    node_parent,
    seg_lengths,
):
    tok_rows = tokens.shape[0]
    mine = lax.axis_index("req")
    n_mlp = lax.axis_size("mlp")
    position_group = lax.axis_index("mlp")
    node_dev = prefix_kv.shape[1]
    seg_slot = prefix_kv.shape[2]
    share = seg_slot // n_mlp
    level_zero = node_parent[leaf_parent]
    n_requests = leaf_parent.shape[0]
    all_lengths = jnp.stack(
        [seg_lengths[0][level_zero], seg_lengths[1][leaf_parent], seg_lengths[2, :n_requests]]
    )
    my_lengths = lax.dynamic_index_in_dim(all_lengths, mine, 1, keepdims=False)
    len_zero = my_lengths[0]
    len_one = my_lengths[1]
    total = len_zero + len_one + my_lengths[2]

    ff_cols = w_gate.shape[1]
    packed = lax.all_gather(
        jnp.concatenate([w_gate, w_up, w_down], 1), "req", axis=0, tiled=True
    )
    down_full = packed[:, 2 * ff_cols :]

    wanted = jnp.stack([level_zero, leaf_parent], 1)
    local_slot = wanted % node_dev
    my_rows = lax.dynamic_slice_in_dim(prefix_kv, position_group * share, share, 2)
    outgoing = my_rows[jnp.arange(2)[None, :], local_slot]
    arrived = lax.all_to_all(outgoing, "req", split_axis=0, concat_axis=0, tiled=True)
    owners = wanted[mine] // node_dev
    my_part = arrived[owners, jnp.arange(2)]
    levels = lax.all_gather(my_part, "mlp", axis=1, tiled=True)

    query_at = total + position_group * tok_rows + jnp.arange(tok_rows, dtype=jnp.int32)
    normed = rms_scale(tokens, attn_gain).astype(jnp.bfloat16)
    query_full = jnp.dot(normed, w_query, preferred_element_type=jnp.float32)
    keyval_full = jnp.dot(normed, w_keyval, preferred_element_type=jnp.float32)
    half_dim = HD // 2
    freqs = 10000.0 ** (-jnp.arange(half_dim, dtype=jnp.float32) / half_dim)
    angles = query_at.astype(jnp.float32)[:, None] * jnp.concatenate([freqs, freqs])[None, :]
    cosine = jnp.cos(angles)
    sine = jnp.sin(angles) * jnp.where(jnp.arange(HD) < half_dim, -1.0, 1.0)
    raw_keys = keyval_full[:, :HD]
    swapped = jnp.concatenate([raw_keys[:, half_dim:], raw_keys[:, :half_dim]], 1)
    new_keys = (raw_keys * cosine + swapped * sine).astype(jnp.bfloat16)
    new_vals = keyval_full[:, HD:].astype(jnp.bfloat16)
    new_keyval = jnp.concatenate([new_keys, new_vals], 1)
    back = WINDOW // tok_rows
    new_keyval, arrived = lax.optimization_barrier((new_keyval, arrived))
    blocks = [
        lax.ppermute(new_keyval, "mlp", [(i, (i + shift) % n_mlp) for i in range(n_mlp)])
        for shift in range(back, 0, -1)
    ]
    sources = jnp.concatenate([levels[0], levels[1], own_prefix[0]] + blocks + [new_keyval], 0)
    span = (back + 1) * tok_rows
    first = total + position_group * tok_rows - WINDOW
    row = jnp.arange(span, dtype=jnp.int32)
    key_at = first + row
    len_cut = len_zero + len_one
    source_row = jnp.where(
        key_at < len_zero,
        key_at,
        jnp.where(
            key_at < len_cut,
            key_at - len_zero + seg_slot,
            jnp.where(key_at < total, key_at - len_cut + 2 * seg_slot, row + 3 * seg_slot),
        ),
    )
    window = jnp.take(sources, source_row, axis=0, mode="clip")
    where = jnp.stack([total + position_group * tok_rows, first]).astype(jnp.int32)
    context = attend_window(query_full, cosine, sine, window, where)
    attn_out = jnp.dot(context, w_out, preferred_element_type=jnp.float32)
    resid = (tokens.astype(jnp.float32) + attn_out).astype(jnp.bfloat16)
    ffn_in = rms_scale(resid, ffn_gain).astype(jnp.bfloat16)
    all_rows = lax.all_gather(ffn_in, "mlp", axis=0, tiled=True)
    gate_up = jnp.dot(all_rows, packed[:, : 2 * ff_cols], preferred_element_type=jnp.float32)
    gate = gate_up[:, :ff_cols]
    upward = gate_up[:, ff_cols:]
    hidden = (jax.nn.gelu(gate, approximate=True) * upward).astype(jnp.bfloat16)
    summed = lax.psum_scatter(
        lax.dot_general(
            hidden, down_full, (((1,), (1,)), ((), ())), preferred_element_type=jnp.float32
        ).astype(jnp.bfloat16),
        "mlp",
        scatter_dimension=0,
        tiled=True,
    ).astype(jnp.float32)
    return (resid.astype(jnp.float32) + summed).astype(jnp.bfloat16)


def solution(mesh):
    return jax.shard_map(
        body,
        mesh=mesh,
        in_specs=(
            P(("req", "mlp"), None),
            P(),
            P(),
            P(),
            P(),
            P(),
            P("req", "mlp"),
            P("req", "mlp"),
            P("req", "mlp"),
            P(None, "req", None, None),
            P("req", None, None),
            P(),
            P(),
            P(),
        ),
        out_specs=P(("req", "mlp"), None),
        check_vma=False,
    )
```

```python
import jax
import jax.numpy as jnp
from jax import lax
from jax.experimental import pallas as pl
from jax.experimental.pallas import tpu as pltpu
from jax.sharding import PartitionSpec as P

HEADS = 12
HD = 128
WINDOW = 1024


EPS = 1e-06


def rms_scale(values, gain):
    wide = values.astype(jnp.float32)
    return wide * lax.rsqrt(jnp.mean(wide * wide, axis=-1, keepdims=True) + EPS) * gain


def rotate(values, where_at):
    half_dim = values.shape[-1] // 2
    freqs = 10000.0 ** (-jnp.arange(half_dim, dtype=jnp.float32) / half_dim)
    angles = where_at.astype(jnp.float32)[:, None] * freqs[None, :]
    cosine = jnp.cos(angles)
    sine = jnp.sin(angles)
    cos_both = jnp.concatenate([cosine, cosine], -1)[:, None, :]
    sin_signed = jnp.concatenate([-sine, sine], -1)[:, None, :]
    swapped = jnp.concatenate([values[..., half_dim:], values[..., :half_dim]], -1)
    return values * cos_both + swapped * sin_signed


def _attend_kernel(where_ref, q_ref, cos_ref, sin_ref, kv_ref, o_ref):
    keys = kv_ref[:, :HD]
    vals = kv_ref[:, HD:]
    cosine = cos_ref[...]
    sine = sin_ref[...]
    shape = (q_ref.shape[0], kv_ref.shape[0])
    query_at = where_ref[0] + lax.broadcasted_iota(jnp.int32, shape, 0)
    key_at = where_ref[1] + lax.broadcasted_iota(jnp.int32, shape, 1)
    spacing = query_at - key_at
    allowed = (key_at >= 0) & (spacing >= 0) & (spacing < WINDOW)
    bias = jnp.where(allowed, 0.0, -jnp.inf).astype(jnp.float32)
    for head in range(q_ref.shape[1] // HD):
        cols = pl.ds(head * HD, HD)
        raw = q_ref[:, cols]
        turned = raw * cosine + pltpu.roll(raw, HD // 2, 1) * sine
        query = (turned * HD ** (-0.5)).astype(jnp.bfloat16)
        scores = lax.dot_general(
            query, keys, (((1,), (1,)), ((), ())), preferred_element_type=jnp.float32
        )
        scores = scores + bias
        top = jnp.max(scores, axis=1, keepdims=True)
        weights = jnp.exp(scores - top)
        denom = jnp.sum(weights, axis=1, keepdims=True)
        mixed = jnp.dot(weights.astype(jnp.bfloat16), vals, preferred_element_type=jnp.float32)
        o_ref[:, cols] = (mixed / denom).astype(o_ref.dtype)


def attend_window(query_full, cosine, sine, window, where, heads_per_step=4):
    rows, width = query_full.shape
    span = window.shape[0]
    step_cols = heads_per_step * HD
    return pl.pallas_call(
        _attend_kernel,
        grid_spec=pltpu.PrefetchScalarGridSpec(
            num_scalar_prefetch=1,
            grid=(width // step_cols,),
            in_specs=[
                pl.BlockSpec((rows, step_cols), lambda h, w: (0, h)),
                pl.BlockSpec((rows, HD), lambda h, w: (0, 0)),
                pl.BlockSpec((rows, HD), lambda h, w: (0, 0)),
                pl.BlockSpec((span, 2 * HD), lambda h, w: (0, 0)),
            ],
            out_specs=pl.BlockSpec((rows, step_cols), lambda h, w: (0, h)),
        ),
        out_shape=jax.ShapeDtypeStruct((rows, width), jnp.bfloat16),
    )(where, query_full, cosine, sine, window)


def body(
    tokens,
    attn_gain,
    w_query,
    w_keyval,
    w_out,
    ffn_gain,
    w_gate,
    w_up,
    w_down,
    prefix_kv,
    own_prefix,
    leaf_parent,
    node_parent,
    seg_lengths,
):
    tok_rows = tokens.shape[0]
    mine = lax.axis_index("req")
    n_mlp = lax.axis_size("mlp")
    position_group = lax.axis_index("mlp")
    node_dev = prefix_kv.shape[1]
    seg_slot = prefix_kv.shape[2]
    share = seg_slot // n_mlp
    level_zero = node_parent[leaf_parent]
    n_requests = leaf_parent.shape[0]
    all_lengths = jnp.stack(
        [seg_lengths[0][level_zero], seg_lengths[1][leaf_parent], seg_lengths[2, :n_requests]]
    )
    my_lengths = lax.dynamic_index_in_dim(all_lengths, mine, 1, keepdims=False)
    len_zero = my_lengths[0]
    len_one = my_lengths[1]
    total = len_zero + len_one + my_lengths[2]

    ff_cols = w_gate.shape[1]
    packed = lax.all_gather(
        jnp.concatenate([w_gate, w_up, w_down], 1), "req", axis=0, tiled=True
    )
    down_full = packed[:, 2 * ff_cols :]

    wanted = jnp.stack([level_zero, leaf_parent], 1)
    local_slot = wanted % node_dev
    my_rows = lax.dynamic_slice_in_dim(prefix_kv, position_group * share, share, 2)
    outgoing = my_rows[jnp.arange(2)[None, :], local_slot]
    arrived = lax.all_to_all(outgoing, "req", split_axis=0, concat_axis=0, tiled=True)
    owners = wanted[mine] // node_dev
    my_part = arrived[owners, jnp.arange(2)]
    fanned = jnp.broadcast_to(my_part[None], (n_mlp,) + my_part.shape)
    levels = lax.all_to_all(fanned, "mlp", split_axis=0, concat_axis=0, tiled=True)
    levels = jnp.swapaxes(levels, 0, 1).reshape(2, seg_slot, my_part.shape[-1])

    query_at = total + position_group * tok_rows + jnp.arange(tok_rows, dtype=jnp.int32)
    normed = rms_scale(tokens, attn_gain).astype(jnp.bfloat16)
    query_full = jnp.dot(normed, w_query, preferred_element_type=jnp.float32)
    keyval_full = jnp.dot(normed, w_keyval, preferred_element_type=jnp.float32)
    half_dim = HD // 2
    freqs = 10000.0 ** (-jnp.arange(half_dim, dtype=jnp.float32) / half_dim)
    angles = query_at.astype(jnp.float32)[:, None] * jnp.concatenate([freqs, freqs])[None, :]
    cosine = jnp.cos(angles)
    sine = jnp.sin(angles) * jnp.where(jnp.arange(HD) < half_dim, -1.0, 1.0)
    raw_keys = keyval_full[:, :HD]
    swapped = jnp.concatenate([raw_keys[:, half_dim:], raw_keys[:, :half_dim]], 1)
    new_keys = (raw_keys * cosine + swapped * sine).astype(jnp.bfloat16)
    new_vals = keyval_full[:, HD:].astype(jnp.bfloat16)
    new_keyval = jnp.concatenate([new_keys, new_vals], 1)
    back = WINDOW // tok_rows
    new_keyval, arrived = lax.optimization_barrier((new_keyval, arrived))
    blocks = [
        lax.ppermute(new_keyval, "mlp", [(i, (i + shift) % n_mlp) for i in range(n_mlp)])
        for shift in range(back, 0, -1)
    ]
    sources = jnp.concatenate([levels[0], levels[1], own_prefix[0]] + blocks + [new_keyval], 0)
    span = (back + 1) * tok_rows
    first = total + position_group * tok_rows - WINDOW
    row = jnp.arange(span, dtype=jnp.int32)
    key_at = first + row
    len_cut = len_zero + len_one
    source_row = jnp.where(
        key_at < len_zero,
        key_at,
        jnp.where(
            key_at < len_cut,
            key_at - len_zero + seg_slot,
            jnp.where(key_at < total, key_at - len_cut + 2 * seg_slot, row + 3 * seg_slot),
        ),
    )
    window = jnp.take(sources, source_row, axis=0, mode="clip")
    where = jnp.stack([total + position_group * tok_rows, first]).astype(jnp.int32)
    context = attend_window(query_full, cosine, sine, window, where)
    attn_out = jnp.dot(context, w_out, preferred_element_type=jnp.float32)
    resid = (tokens.astype(jnp.float32) + attn_out).astype(jnp.bfloat16)
    ffn_in = rms_scale(resid, ffn_gain).astype(jnp.bfloat16)
    all_rows = lax.all_gather(ffn_in, "mlp", axis=0, tiled=True)
    gate_up = jnp.dot(all_rows, packed[:, : 2 * ff_cols], preferred_element_type=jnp.float32)
    gate = gate_up[:, :ff_cols]
    upward = gate_up[:, ff_cols:]
    hidden = (jax.nn.gelu(gate, approximate=True) * upward).astype(jnp.bfloat16)
    summed = lax.psum_scatter(
        lax.dot_general(
            hidden, down_full, (((1,), (1,)), ((), ())), preferred_element_type=jnp.float32
        ).astype(jnp.bfloat16),
        "mlp",
        scatter_dimension=0,
        tiled=True,
    ).astype(jnp.float32)
    return (resid.astype(jnp.float32) + summed).astype(jnp.bfloat16)


def solution(mesh):
    return jax.shard_map(
        body,
        mesh=mesh,
        in_specs=(
            P(("req", "mlp"), None),
            P(),
            P(),
            P(),
            P(),
            P(),
            P("req", "mlp"),
            P("req", "mlp"),
            P("req", "mlp"),
            P(None, "req", None, None),
            P("req", None, None),
            P(),
            P(),
            P(),
        ),
        out_specs=P(("req", "mlp"), None),
        check_vma=False,
    )
```

```python
import jax
import jax.numpy as jnp
from jax import lax
from jax.experimental import pallas as pl
from jax.experimental.pallas import tpu as pltpu
from jax.sharding import PartitionSpec as P

HEADS = 12
HD = 128
WINDOW = 1024


EPS = 1e-06


def rms_scale(values, gain):
    wide = values.astype(jnp.float32)
    return wide * lax.rsqrt(jnp.mean(wide * wide, axis=-1, keepdims=True) + EPS) * gain


def rotate(values, where_at):
    half_dim = values.shape[-1] // 2
    freqs = 10000.0 ** (-jnp.arange(half_dim, dtype=jnp.float32) / half_dim)
    angles = where_at.astype(jnp.float32)[:, None] * freqs[None, :]
    cosine = jnp.cos(angles)
    sine = jnp.sin(angles)
    cos_both = jnp.concatenate([cosine, cosine], -1)[:, None, :]
    sin_signed = jnp.concatenate([-sine, sine], -1)[:, None, :]
    swapped = jnp.concatenate([values[..., half_dim:], values[..., :half_dim]], -1)
    return values * cos_both + swapped * sin_signed


def _attend_kernel(where_ref, q_ref, cos_ref, sin_ref, kv_ref, o_ref):
    keys = kv_ref[:, :HD]
    vals = kv_ref[:, HD:]
    cosine = cos_ref[...]
    sine = sin_ref[...]
    shape = (q_ref.shape[0], kv_ref.shape[0])
    query_at = where_ref[0] + lax.broadcasted_iota(jnp.int32, shape, 0)
    key_at = where_ref[1] + lax.broadcasted_iota(jnp.int32, shape, 1)
    spacing = query_at - key_at
    allowed = (key_at >= 0) & (spacing >= 0) & (spacing < WINDOW)
    bias = jnp.where(allowed, 0.0, -jnp.inf).astype(jnp.float32)
    for head in range(q_ref.shape[1] // HD):
        cols = pl.ds(head * HD, HD)
        raw = q_ref[:, cols]
        turned = raw * cosine + pltpu.roll(raw, HD // 2, 1) * sine
        query = (turned * HD ** (-0.5)).astype(jnp.bfloat16)
        scores = lax.dot_general(
            query, keys, (((1,), (1,)), ((), ())), preferred_element_type=jnp.float32
        )
        scores = scores + bias
        top = jnp.max(scores, axis=1, keepdims=True)
        weights = jnp.exp(scores - top)
        denom = jnp.sum(weights, axis=1, keepdims=True)
        mixed = jnp.dot(weights.astype(jnp.bfloat16), vals, preferred_element_type=jnp.float32)
        o_ref[:, cols] = (mixed / denom).astype(o_ref.dtype)


def attend_window(query_full, cosine, sine, window, where, heads_per_step=4):
    rows, width = query_full.shape
    span = window.shape[0]
    step_cols = heads_per_step * HD
    return pl.pallas_call(
        _attend_kernel,
        grid_spec=pltpu.PrefetchScalarGridSpec(
            num_scalar_prefetch=1,
            grid=(width // step_cols,),
            in_specs=[
                pl.BlockSpec((rows, step_cols), lambda h, w: (0, h)),
                pl.BlockSpec((rows, HD), lambda h, w: (0, 0)),
                pl.BlockSpec((rows, HD), lambda h, w: (0, 0)),
                pl.BlockSpec((span, 2 * HD), lambda h, w: (0, 0)),
            ],
            out_specs=pl.BlockSpec((rows, step_cols), lambda h, w: (0, h)),
        ),
        out_shape=jax.ShapeDtypeStruct((rows, width), jnp.bfloat16),
    )(where, query_full, cosine, sine, window)


def body(
    tokens,
    attn_gain,
    w_query,
    w_keyval,
    w_out,
    ffn_gain,
    w_gate,
    w_up,
    w_down,
    prefix_kv,
    own_prefix,
    leaf_parent,
    node_parent,
    seg_lengths,
):
    tok_rows = tokens.shape[0]
    mine = lax.axis_index("req")
    n_mlp = lax.axis_size("mlp")
    position_group = lax.axis_index("mlp")
    node_dev = prefix_kv.shape[1]
    seg_slot = prefix_kv.shape[2]
    share = seg_slot // n_mlp
    level_zero = node_parent[leaf_parent]
    n_requests = leaf_parent.shape[0]
    all_lengths = jnp.stack(
        [seg_lengths[0][level_zero], seg_lengths[1][leaf_parent], seg_lengths[2, :n_requests]]
    )
    my_lengths = lax.dynamic_index_in_dim(all_lengths, mine, 1, keepdims=False)
    len_zero = my_lengths[0]
    len_one = my_lengths[1]
    total = len_zero + len_one + my_lengths[2]

    ff_cols = w_gate.shape[1]
    packed = lax.all_gather(
        jnp.concatenate([w_gate, w_up, w_down], 1), "req", axis=0, tiled=True
    )
    down_full = packed[:, 2 * ff_cols :]

    wanted = jnp.stack([level_zero, leaf_parent], 1)
    local_slot = wanted % node_dev
    my_rows = lax.dynamic_slice_in_dim(prefix_kv, position_group * share, share, 2)
    outgoing = my_rows[jnp.arange(2)[None, :], local_slot]
    arrived = lax.all_to_all(outgoing, "req", split_axis=0, concat_axis=0, tiled=True)
    owners = wanted[mine] // node_dev
    my_part = arrived[owners, jnp.arange(2)]
    levels = lax.all_gather(my_part, "mlp", axis=1, tiled=True)

    query_at = total + position_group * tok_rows + jnp.arange(tok_rows, dtype=jnp.int32)
    normed = rms_scale(tokens, attn_gain).astype(jnp.bfloat16)
    query_full = jnp.dot(normed, w_query, preferred_element_type=jnp.float32)
    keyval_full = jnp.dot(normed, w_keyval, preferred_element_type=jnp.float32)
    half_dim = HD // 2
    freqs = 10000.0 ** (-jnp.arange(half_dim, dtype=jnp.float32) / half_dim)
    angles = query_at.astype(jnp.float32)[:, None] * jnp.concatenate([freqs, freqs])[None, :]
    cosine = jnp.cos(angles)
    sine = jnp.sin(angles) * jnp.where(jnp.arange(HD) < half_dim, -1.0, 1.0)
    raw_keys = keyval_full[:, :HD]
    swapped = jnp.concatenate([raw_keys[:, half_dim:], raw_keys[:, :half_dim]], 1)
    new_keys = (raw_keys * cosine + swapped * sine).astype(jnp.bfloat16)
    new_vals = keyval_full[:, HD:].astype(jnp.bfloat16)
    new_keyval = jnp.concatenate([new_keys, new_vals], 1)
    back = WINDOW // tok_rows
    new_keyval, query_full = lax.optimization_barrier((new_keyval, query_full))
    blocks = [
        lax.ppermute(new_keyval, "mlp", [(i, (i + shift) % n_mlp) for i in range(n_mlp)])
        for shift in range(back, 0, -1)
    ]
    sources = jnp.concatenate([levels[0], levels[1], own_prefix[0]] + blocks + [new_keyval], 0)
    span = (back + 1) * tok_rows
    first = total + position_group * tok_rows - WINDOW
    row = jnp.arange(span, dtype=jnp.int32)
    key_at = first + row
    len_cut = len_zero + len_one
    source_row = jnp.where(
        key_at < len_zero,
        key_at,
        jnp.where(
            key_at < len_cut,
            key_at - len_zero + seg_slot,
            jnp.where(key_at < total, key_at - len_cut + 2 * seg_slot, row + 3 * seg_slot),
        ),
    )
    window = jnp.take(sources, source_row, axis=0, mode="clip")
    where = jnp.stack([total + position_group * tok_rows, first]).astype(jnp.int32)
    context = attend_window(query_full, cosine, sine, window, where)
    attn_out = jnp.dot(context, w_out, preferred_element_type=jnp.float32)
    resid = (tokens.astype(jnp.float32) + attn_out).astype(jnp.bfloat16)
    ffn_in = rms_scale(resid, ffn_gain).astype(jnp.bfloat16)
    all_rows = lax.all_gather(ffn_in, "mlp", axis=0, tiled=True)
    gate_up = jnp.dot(all_rows, packed[:, : 2 * ff_cols], preferred_element_type=jnp.float32)
    gate = gate_up[:, :ff_cols]
    upward = gate_up[:, ff_cols:]
    hidden = (jax.nn.gelu(gate, approximate=True) * upward).astype(jnp.bfloat16)
    summed = lax.psum_scatter(
        lax.dot_general(
            hidden, down_full, (((1,), (1,)), ((), ())), preferred_element_type=jnp.float32
        ).astype(jnp.bfloat16),
        "mlp",
        scatter_dimension=0,
        tiled=True,
    ).astype(jnp.float32)
    return (resid.astype(jnp.float32) + summed).astype(jnp.bfloat16)


def solution(mesh):
    return jax.shard_map(
        body,
        mesh=mesh,
        in_specs=(
            P(("req", "mlp"), None),
            P(),
            P(),
            P(),
            P(),
            P(),
            P("req", "mlp"),
            P("req", "mlp"),
            P("req", "mlp"),
            P(None, "req", None, None),
            P("req", None, None),
            P(),
            P(),
            P(),
        ),
        out_specs=P(("req", "mlp"), None),
        check_vma=False,
    )
```

```python
import jax
import jax.numpy as jnp
from jax import lax
from jax.experimental import pallas as pl
from jax.experimental.pallas import tpu as pltpu
from jax.sharding import PartitionSpec as P

HEADS = 12
HD = 128
WINDOW = 1024


EPS = 1e-06


def rms_scale(values, gain):
    wide = values.astype(jnp.float32)
    return wide * lax.rsqrt(jnp.mean(wide * wide, axis=-1, keepdims=True) + EPS) * gain


def rotate(values, where_at):
    half_dim = values.shape[-1] // 2
    freqs = 10000.0 ** (-jnp.arange(half_dim, dtype=jnp.float32) / half_dim)
    angles = where_at.astype(jnp.float32)[:, None] * freqs[None, :]
    cosine = jnp.cos(angles)
    sine = jnp.sin(angles)
    cos_both = jnp.concatenate([cosine, cosine], -1)[:, None, :]
    sin_signed = jnp.concatenate([-sine, sine], -1)[:, None, :]
    swapped = jnp.concatenate([values[..., half_dim:], values[..., :half_dim]], -1)
    return values * cos_both + swapped * sin_signed


def _attend_kernel(where_ref, q_ref, cos_ref, sin_ref, kv_ref, o_ref):
    keys = kv_ref[:, :HD]
    vals = kv_ref[:, HD:]
    cosine = cos_ref[...]
    sine = sin_ref[...]
    shape = (q_ref.shape[0], kv_ref.shape[0])
    query_at = where_ref[0] + lax.broadcasted_iota(jnp.int32, shape, 0)
    key_at = where_ref[1] + lax.broadcasted_iota(jnp.int32, shape, 1)
    spacing = query_at - key_at
    allowed = (key_at >= 0) & (spacing >= 0) & (spacing < WINDOW)
    bias = jnp.where(allowed, 0.0, -jnp.inf).astype(jnp.float32)
    for head in range(q_ref.shape[1] // HD):
        cols = pl.ds(head * HD, HD)
        raw = q_ref[:, cols]
        turned = raw * cosine + pltpu.roll(raw, HD // 2, 1) * sine
        query = (turned * HD ** (-0.5)).astype(jnp.bfloat16)
        scores = lax.dot_general(
            query, keys, (((1,), (1,)), ((), ())), preferred_element_type=jnp.float32
        )
        scores = scores + bias
        top = jnp.max(scores, axis=1, keepdims=True)
        weights = jnp.exp(scores - top)
        denom = jnp.sum(weights, axis=1, keepdims=True)
        mixed = jnp.dot(weights.astype(jnp.bfloat16), vals, preferred_element_type=jnp.float32)
        o_ref[:, cols] = (mixed / denom).astype(o_ref.dtype)


def attend_window(query_full, cosine, sine, window, where, heads_per_step=4):
    rows, width = query_full.shape
    span = window.shape[0]
    step_cols = heads_per_step * HD
    return pl.pallas_call(
        _attend_kernel,
        grid_spec=pltpu.PrefetchScalarGridSpec(
            num_scalar_prefetch=1,
            grid=(width // step_cols,),
            in_specs=[
                pl.BlockSpec((rows, step_cols), lambda h, w: (0, h)),
                pl.BlockSpec((rows, HD), lambda h, w: (0, 0)),
                pl.BlockSpec((rows, HD), lambda h, w: (0, 0)),
                pl.BlockSpec((span, 2 * HD), lambda h, w: (0, 0)),
            ],
            out_specs=pl.BlockSpec((rows, step_cols), lambda h, w: (0, h)),
        ),
        out_shape=jax.ShapeDtypeStruct((rows, width), jnp.bfloat16),
    )(where, query_full, cosine, sine, window)


def _ffn_kernel(x_ref, w_ref, o_ref):
    rows = x_ref[...]
    width = w_ref.shape[1] // 3
    gate = jnp.dot(rows, w_ref[:, :width], preferred_element_type=jnp.float32)
    upward = jnp.dot(rows, w_ref[:, width : 2 * width], preferred_element_type=jnp.float32)
    hidden = (jax.nn.gelu(gate, approximate=True) * upward).astype(jnp.bfloat16)
    partial_down = lax.dot_general(
        hidden, w_ref[:, 2 * width :], (((1,), (1,)), ((), ())), preferred_element_type=jnp.float32
    )
    o_ref[...] = partial_down.astype(o_ref.dtype)


def ffn_block(all_rows, packed, block_rows=512):
    rows, model = all_rows.shape
    return pl.pallas_call(
        _ffn_kernel,
        grid=(rows // block_rows,),
        in_specs=[
            pl.BlockSpec((block_rows, model), lambda i: (i, 0)),
            pl.BlockSpec(packed.shape, lambda i: (0, 0)),
        ],
        out_specs=pl.BlockSpec((block_rows, model), lambda i: (i, 0)),
        out_shape=jax.ShapeDtypeStruct((rows, model), jnp.bfloat16),
    )(all_rows, packed)


def body(
    tokens,
    attn_gain,
    w_query,
    w_keyval,
    w_out,
    ffn_gain,
    w_gate,
    w_up,
    w_down,
    prefix_kv,
    own_prefix,
    leaf_parent,
    node_parent,
    seg_lengths,
):
    tok_rows = tokens.shape[0]
    mine = lax.axis_index("req")
    n_mlp = lax.axis_size("mlp")
    position_group = lax.axis_index("mlp")
    node_dev = prefix_kv.shape[1]
    seg_slot = prefix_kv.shape[2]
    share = seg_slot // n_mlp
    level_zero = node_parent[leaf_parent]
    n_requests = leaf_parent.shape[0]
    all_lengths = jnp.stack(
        [seg_lengths[0][level_zero], seg_lengths[1][leaf_parent], seg_lengths[2, :n_requests]]
    )
    my_lengths = lax.dynamic_index_in_dim(all_lengths, mine, 1, keepdims=False)
    len_zero = my_lengths[0]
    len_one = my_lengths[1]
    total = len_zero + len_one + my_lengths[2]

    ff_cols = w_gate.shape[1]
    lanes = -(-ff_cols // 128) * 128
    padded = [jnp.pad(part, ((0, 0), (0, lanes - ff_cols))) for part in (w_gate, w_up, w_down)]
    packed = lax.all_gather(jnp.concatenate(padded, 1), "req", axis=0, tiled=True)

    wanted = jnp.stack([level_zero, leaf_parent], 1)
    local_slot = wanted % node_dev
    my_rows = lax.dynamic_slice_in_dim(prefix_kv, position_group * share, share, 2)
    outgoing = my_rows[jnp.arange(2)[None, :], local_slot]
    arrived = lax.all_to_all(outgoing, "req", split_axis=0, concat_axis=0, tiled=True)
    owners = wanted[mine] // node_dev
    my_part = arrived[owners, jnp.arange(2)]
    levels = lax.all_gather(my_part, "mlp", axis=1, tiled=True)

    query_at = total + position_group * tok_rows + jnp.arange(tok_rows, dtype=jnp.int32)
    normed = rms_scale(tokens, attn_gain).astype(jnp.bfloat16)
    query_full = jnp.dot(normed, w_query, preferred_element_type=jnp.float32)
    keyval_full = jnp.dot(normed, w_keyval, preferred_element_type=jnp.float32)
    half_dim = HD // 2
    freqs = 10000.0 ** (-jnp.arange(half_dim, dtype=jnp.float32) / half_dim)
    angles = query_at.astype(jnp.float32)[:, None] * jnp.concatenate([freqs, freqs])[None, :]
    cosine = jnp.cos(angles)
    sine = jnp.sin(angles) * jnp.where(jnp.arange(HD) < half_dim, -1.0, 1.0)
    raw_keys = keyval_full[:, :HD]
    swapped = jnp.concatenate([raw_keys[:, half_dim:], raw_keys[:, :half_dim]], 1)
    new_keys = (raw_keys * cosine + swapped * sine).astype(jnp.bfloat16)
    new_vals = keyval_full[:, HD:].astype(jnp.bfloat16)
    new_keyval = jnp.concatenate([new_keys, new_vals], 1)
    back = WINDOW // tok_rows
    new_keyval, query_full = lax.optimization_barrier((new_keyval, query_full))
    blocks = [
        lax.ppermute(new_keyval, "mlp", [(i, (i + shift) % n_mlp) for i in range(n_mlp)])
        for shift in range(back, 0, -1)
    ]
    sources = jnp.concatenate([levels[0], levels[1], own_prefix[0]] + blocks + [new_keyval], 0)
    span = (back + 1) * tok_rows
    first = total + position_group * tok_rows - WINDOW
    row = jnp.arange(span, dtype=jnp.int32)
    key_at = first + row
    len_cut = len_zero + len_one
    source_row = jnp.where(
        key_at < len_zero,
        key_at,
        jnp.where(
            key_at < len_cut,
            key_at - len_zero + seg_slot,
            jnp.where(key_at < total, key_at - len_cut + 2 * seg_slot, row + 3 * seg_slot),
        ),
    )
    window = jnp.take(sources, source_row, axis=0, mode="clip")
    where = jnp.stack([total + position_group * tok_rows, first]).astype(jnp.int32)
    context = attend_window(query_full, cosine, sine, window, where)
    attn_out = jnp.dot(context, w_out, preferred_element_type=jnp.float32)
    resid = (tokens.astype(jnp.float32) + attn_out).astype(jnp.bfloat16)
    ffn_in = rms_scale(resid, ffn_gain).astype(jnp.bfloat16)
    all_rows = lax.all_gather(ffn_in, "mlp", axis=0, tiled=True)
    partial_down = ffn_block(all_rows, packed)
    summed = lax.psum_scatter(
        partial_down, "mlp", scatter_dimension=0, tiled=True
    ).astype(jnp.float32)
    return (resid.astype(jnp.float32) + summed).astype(jnp.bfloat16)


def solution(mesh):
    return jax.shard_map(
        body,
        mesh=mesh,
        in_specs=(
            P(("req", "mlp"), None),
            P(),
            P(),
            P(),
            P(),
            P(),
            P("req", "mlp"),
            P("req", "mlp"),
            P("req", "mlp"),
            P(None, "req", None, None),
            P("req", None, None),
            P(),
            P(),
            P(),
        ),
        out_specs=P(("req", "mlp"), None),
        check_vma=False,
    )
```

```python
import jax
import jax.numpy as jnp
from jax import lax
from jax.experimental import pallas as pl
from jax.experimental.pallas import tpu as pltpu
from jax.sharding import PartitionSpec as P

HEADS = 12
HD = 128
WINDOW = 1024


EPS = 1e-06


def rms_scale(values, gain):
    wide = values.astype(jnp.float32)
    return wide * lax.rsqrt(jnp.mean(wide * wide, axis=-1, keepdims=True) + EPS) * gain


def rotate(values, where_at):
    half_dim = values.shape[-1] // 2
    freqs = 10000.0 ** (-jnp.arange(half_dim, dtype=jnp.float32) / half_dim)
    angles = where_at.astype(jnp.float32)[:, None] * freqs[None, :]
    cosine = jnp.cos(angles)
    sine = jnp.sin(angles)
    cos_both = jnp.concatenate([cosine, cosine], -1)[:, None, :]
    sin_signed = jnp.concatenate([-sine, sine], -1)[:, None, :]
    swapped = jnp.concatenate([values[..., half_dim:], values[..., :half_dim]], -1)
    return values * cos_both + swapped * sin_signed


def _attend_kernel(where_ref, q_ref, cos_ref, sin_ref, kv_ref, o_ref):
    keys = kv_ref[:, :HD]
    vals = kv_ref[:, HD:]
    cosine = cos_ref[...]
    sine = sin_ref[...]
    shape = (q_ref.shape[0], kv_ref.shape[0])
    query_at = where_ref[0] + lax.broadcasted_iota(jnp.int32, shape, 0)
    key_at = where_ref[1] + lax.broadcasted_iota(jnp.int32, shape, 1)
    spacing = query_at - key_at
    allowed = (key_at >= 0) & (spacing >= 0) & (spacing < WINDOW)
    bias = jnp.where(allowed, 0.0, -jnp.inf).astype(jnp.float32)
    for head in range(q_ref.shape[1] // HD):
        cols = pl.ds(head * HD, HD)
        raw = q_ref[:, cols]
        turned = raw * cosine + pltpu.roll(raw, HD // 2, 1) * sine
        query = (turned * HD ** (-0.5)).astype(jnp.bfloat16)
        scores = lax.dot_general(
            query, keys, (((1,), (1,)), ((), ())), preferred_element_type=jnp.float32
        )
        scores = scores + bias
        top = jnp.max(scores, axis=1, keepdims=True)
        weights = jnp.exp(scores - top)
        denom = jnp.sum(weights, axis=1, keepdims=True)
        mixed = jnp.dot(weights.astype(jnp.bfloat16), vals, preferred_element_type=jnp.float32)
        o_ref[:, cols] = (mixed / denom).astype(o_ref.dtype)


def attend_window(query_full, cosine, sine, window, where, heads_per_step=12):
    rows, width = query_full.shape
    span = window.shape[0]
    step_cols = heads_per_step * HD
    return pl.pallas_call(
        _attend_kernel,
        grid_spec=pltpu.PrefetchScalarGridSpec(
            num_scalar_prefetch=1,
            grid=(width // step_cols,),
            in_specs=[
                pl.BlockSpec((rows, step_cols), lambda h, w: (0, h)),
                pl.BlockSpec((rows, HD), lambda h, w: (0, 0)),
                pl.BlockSpec((rows, HD), lambda h, w: (0, 0)),
                pl.BlockSpec((span, 2 * HD), lambda h, w: (0, 0)),
            ],
            out_specs=pl.BlockSpec((rows, step_cols), lambda h, w: (0, h)),
        ),
        out_shape=jax.ShapeDtypeStruct((rows, width), jnp.bfloat16),
    )(where, query_full, cosine, sine, window)


def body(
    tokens,
    attn_gain,
    w_query,
    w_keyval,
    w_out,
    ffn_gain,
    w_gate,
    w_up,
    w_down,
    prefix_kv,
    own_prefix,
    leaf_parent,
    node_parent,
    seg_lengths,
):
    tok_rows = tokens.shape[0]
    mine = lax.axis_index("req")
    n_mlp = lax.axis_size("mlp")
    position_group = lax.axis_index("mlp")
    node_dev = prefix_kv.shape[1]
    seg_slot = prefix_kv.shape[2]
    share = seg_slot // n_mlp
    level_zero = node_parent[leaf_parent]
    n_requests = leaf_parent.shape[0]
    all_lengths = jnp.stack(
        [seg_lengths[0][level_zero], seg_lengths[1][leaf_parent], seg_lengths[2, :n_requests]]
    )
    my_lengths = lax.dynamic_index_in_dim(all_lengths, mine, 1, keepdims=False)
    len_zero = my_lengths[0]
    len_one = my_lengths[1]
    total = len_zero + len_one + my_lengths[2]

    ff_cols = w_gate.shape[1]
    packed = lax.all_gather(
        jnp.concatenate([w_gate, w_up, w_down], 1), "req", axis=0, tiled=True
    )
    down_full = packed[:, 2 * ff_cols :]

    wanted = jnp.stack([level_zero, leaf_parent], 1)
    local_slot = wanted % node_dev
    my_rows = lax.dynamic_slice_in_dim(prefix_kv, position_group * share, share, 2)
    outgoing = my_rows[jnp.arange(2)[None, :], local_slot]
    arrived = lax.all_to_all(outgoing, "req", split_axis=0, concat_axis=0, tiled=True)
    owners = wanted[mine] // node_dev
    my_part = arrived[owners, jnp.arange(2)]
    levels = lax.all_gather(my_part, "mlp", axis=1, tiled=True)

    query_at = total + position_group * tok_rows + jnp.arange(tok_rows, dtype=jnp.int32)
    normed = rms_scale(tokens, attn_gain).astype(jnp.bfloat16)
    query_full = jnp.dot(normed, w_query, preferred_element_type=jnp.float32)
    keyval_full = jnp.dot(normed, w_keyval, preferred_element_type=jnp.float32)
    half_dim = HD // 2
    freqs = 10000.0 ** (-jnp.arange(half_dim, dtype=jnp.float32) / half_dim)
    angles = query_at.astype(jnp.float32)[:, None] * jnp.concatenate([freqs, freqs])[None, :]
    cosine = jnp.cos(angles)
    sine = jnp.sin(angles) * jnp.where(jnp.arange(HD) < half_dim, -1.0, 1.0)
    raw_keys = keyval_full[:, :HD]
    swapped = jnp.concatenate([raw_keys[:, half_dim:], raw_keys[:, :half_dim]], 1)
    new_keys = (raw_keys * cosine + swapped * sine).astype(jnp.bfloat16)
    new_vals = keyval_full[:, HD:].astype(jnp.bfloat16)
    new_keyval = jnp.concatenate([new_keys, new_vals], 1)
    back = WINDOW // tok_rows
    new_keyval, query_full = lax.optimization_barrier((new_keyval, query_full))
    blocks = [
        lax.ppermute(new_keyval, "mlp", [(i, (i + shift) % n_mlp) for i in range(n_mlp)])
        for shift in range(back, 0, -1)
    ]
    sources = jnp.concatenate([levels[0], levels[1], own_prefix[0]] + blocks + [new_keyval], 0)
    span = (back + 1) * tok_rows
    first = total + position_group * tok_rows - WINDOW
    row = jnp.arange(span, dtype=jnp.int32)
    key_at = first + row
    len_cut = len_zero + len_one
    source_row = jnp.where(
        key_at < len_zero,
        key_at,
        jnp.where(
            key_at < len_cut,
            key_at - len_zero + seg_slot,
            jnp.where(key_at < total, key_at - len_cut + 2 * seg_slot, row + 3 * seg_slot),
        ),
    )
    window = jnp.take(sources, source_row, axis=0, mode="clip")
    where = jnp.stack([total + position_group * tok_rows, first]).astype(jnp.int32)
    context = attend_window(query_full, cosine, sine, window, where)
    attn_out = jnp.dot(context, w_out, preferred_element_type=jnp.float32)
    resid = (tokens.astype(jnp.float32) + attn_out).astype(jnp.bfloat16)
    ffn_in = rms_scale(resid, ffn_gain).astype(jnp.bfloat16)
    all_rows = lax.all_gather(ffn_in, "mlp", axis=0, tiled=True)
    gate_up = jnp.dot(all_rows, packed[:, : 2 * ff_cols], preferred_element_type=jnp.float32)
    gate = gate_up[:, :ff_cols]
    upward = gate_up[:, ff_cols:]
    hidden = (jax.nn.gelu(gate, approximate=True) * upward).astype(jnp.bfloat16)
    summed = lax.psum_scatter(
        lax.dot_general(
            hidden, down_full, (((1,), (1,)), ((), ())), preferred_element_type=jnp.float32
        ).astype(jnp.bfloat16),
        "mlp",
        scatter_dimension=0,
        tiled=True,
    ).astype(jnp.float32)
    return (resid.astype(jnp.float32) + summed).astype(jnp.bfloat16)


def solution(mesh):
    return jax.shard_map(
        body,
        mesh=mesh,
        in_specs=(
            P(("req", "mlp"), None),
            P(),
            P(),
            P(),
            P(),
            P(),
            P("req", "mlp"),
            P("req", "mlp"),
            P("req", "mlp"),
            P(None, "req", None, None),
            P("req", None, None),
            P(),
            P(),
            P(),
        ),
        out_specs=P(("req", "mlp"), None),
        check_vma=False,
    )
```
